128 devices in a mesh: expert: 8 (over z, core), ffn: 16 (over x, y).
Axes of the slice: x: 4, y: 4, z: 4, core: 2. Of those that a mesh axis runs over, the one named last changes fastest.
Arguments:
- queries: bfloat16 [512, 4096], P(('expert', 'ffn')), may hold values from -8 to 8
- new_keys: bfloat16 [512, 1024], P(('expert', 'ffn')), may hold values from -4 to 4
- new_values: bfloat16 [512, 1024], P(('expert', 'ffn')), may hold values from -5 to 5
- key_cache: bfloat16 [512, 512, 1024], P(('expert', 'ffn')), may hold values from -4 to 4
- value_cache: bfloat16 [512, 512, 1024], P(('expert', 'ffn')), may hold values from -5 to 5
- lengths: int32 [512], P(('expert', 'ffn')), may hold values from 1 to 512, 65536 in all
- residual: bfloat16 [512, 4096], P('expert', 'ffn'), may hold values from -16 to 16
- out_weight: bfloat16 [4096, 4096], P(None, 'ffn'), may hold values from -0.1875 to 0.1875
- norm_gain: float32 [4096], P('ffn'), may hold values from 0.25 to 1.75
- router: float32 [4096, 8], P('ffn'), may hold values from -0.09375 to 0.09375
- gate_weight: bfloat16 [8, 4096, 8192], P('expert', None, 'ffn'), may hold values from -0.09375 to 0.09375
- up_weight: bfloat16 [8, 4096, 8192], P('expert', None, 'ffn'), may hold values from -0.09375 to 0.09375
- down_weight: bfloat16 [8, 8192, 4096], P('expert', 'ffn'), may hold values from -0.09375 to 0.09375
- routes: int32 [512, 2], P('expert'), may hold values from 0 to 7, all different within a row; in each aligned block of 64 rows (0 to 63, 64 to 127, ...) at most 32 rows name the same one
Outputs:
- layer_out: bfloat16 [512, 4096], P('expert', 'ffn')
The draws below stay inside these ranges and needn't reach their ends.
Inputs may be any that keep to these rules, and one draw needn't show every extreme that they name: The lengths of all 512 requests sum to 65536, and some request has exactly 512. `routes`: A request names two different experts. In each aligned block of 64 requests (the requests of one index of expert) no expert is named by more than 32 requests, a bound that some block reaches.
All inputs are finite; a program needn't handle non-finite values. No bound on the sum of `lengths` on one device may be relied on, other than what follows from the above.
Results may differ from the reference program's by a relative error of at most 0.0065.
Values may be sent and summed in bfloat16 or wider, within the bound.
No kernel may reach another device: no remote copies, remote signals or barrier semaphores. Data moves between devices by JAX's collectives and lax.ppermute only.
A program may use at most 128 MiB of HBM per device.

```python
import math
import jax
import jax.numpy as jnp
import numpy as np
from jax import lax

D = 4096
QH = 32
KVH = 8
HD = 128
FF = 8192
CACHE = 512
EXPERTS = 8
RROW = 64
CAP = 32
R = 512


def base_values(key, shape, bound):
    return jnp.clip(jax.random.normal(key, shape, jnp.float32), -bound, bound)


def draw_queries(key, part):
    values = base_values(jax.random.fold_in(key, 1), (R, KVH, QH // KVH, HD), 4.0)
    return values.reshape(R, QH * HD).astype(jnp.bfloat16)


def draw_key_cache(key, part):
    values = base_values(jax.random.fold_in(key, 2), (R, CACHE, KVH * HD), 4.0)
    return values.astype(jnp.bfloat16)


def draw_new_keys(key, part):
    values = base_values(jax.random.fold_in(key, 3), (R, KVH * HD), 4.0)
    return values.astype(jnp.bfloat16)


def draw_residual(key, part):
    values = base_values(jax.random.fold_in(key, 4), (R, D), 4.0)
    row_scale = jnp.exp(jax.random.uniform(jax.random.fold_in(key, 5), (R, 1), jnp.float32, math.log(0.2), math.log(2.0)))
    rise = 3.0
    column_scale = jnp.power(rise, jnp.arange(D, dtype=jnp.float32) / (D - 1))
    return jnp.clip(values * row_scale * column_scale[None, :], -16.0, 16.0).astype(jnp.bfloat16)


def strengthened(drawn, own_key, source, target, parts, factor):
    def block_of(dim):
        return (jnp.arange(drawn.shape[dim]) // (drawn.shape[dim] // parts)).reshape((-1,) + (1,) * (drawn.ndim - 1 - dim))

    one_side = jax.random.permutation(own_key, parts)[block_of(target)]
    other_side = (block_of(target) + parts // 2) % parts
    return jnp.where((block_of(source) == one_side) | (block_of(source) == other_side), factor * drawn, drawn)


def levels(stream_key, shape, pieces, least, high):
    level = 1.0
    for position, blocks in pieces:
        steps = jax.random.uniform(jax.random.fold_in(jax.random.fold_in(stream_key, 6), position), (blocks,), jnp.float32, least / len(pieces), high / len(pieces))
        level = level * jnp.repeat(jnp.exp(steps), shape[position] // blocks).reshape((-1,) + (1,) * (len(shape) - 1 - position))
    return level


def profile(amount, total, limit, slope):
    portions = [(1 << 20) // math.isqrt(standing ** slope) + 1 for standing in range(2, amount + 1)]
    surplus, counts = total - limit - (amount - 1), [1] * (amount - 1)
    while surplus > 0:
        candidates = [i for i in range(amount - 1) if counts[i] < limit]
        whole, left = sum([portions[i] for i in candidates]), surplus
        for i in candidates:
            addition = min(limit - counts[i], max(1, left * portions[i] // whole), surplus)
            counts[i] = counts[i] + addition
            surplus = surplus - addition
    return np.array([limit] + counts)


def ragged_sizes(rng, count, total, most, slope):
    if count == 2:
        one = jax.random.randint(rng, (), max(1, total - most), min(most, total - 1) + 1)
        return jnp.stack([one, total - one])
    sizes = jnp.asarray(profile(count, total, most, slope), jnp.int32)
    twos = (count - 1) // 2
    donor, taker = sizes[1:1 + 2 * twos:2], sizes[2:2 + 2 * twos:2]
    room = jnp.minimum(donor - 1, most - taker)
    shifted = jax.random.randint(jax.random.fold_in(rng, 1), (twos,), 0, 1 << 20) % (room + 1)
    sizes = sizes.at[1:1 + 2 * twos:2].set(donor - shifted).at[2:2 + 2 * twos:2].set(taker + shifted)
    return sizes[jax.random.permutation(jax.random.fold_in(rng, 2), count)]


def shared_out(key, own, number, rows, count, top, limit, slope):
    sequence = jax.random.permutation(key, count)
    crowded, common = load_shares(count, rows * top, limit, slope, True), load_shares(count, rows * top, limit, slope, False)
    places = jnp.arange(count)

    def named(sizes, offset_by):
        used = int((sizes > 0).sum())
        fixed = max(1, used // 4)
        shifted = fixed + (places - fixed + offset_by * (used - fixed)) % max(1, count - fixed)
        return jnp.zeros((count,), jnp.int32).at[sequence[jnp.where(places < fixed, places, shifted)]].set(jnp.asarray(sizes, jnp.int32))

    sizes = jnp.where(number % 4 == 0, named(crowded, number // 4), named(common, number - number // 4 - 1))
    mixed = jax.random.permutation(jax.random.fold_in(own, 3), count)
    source_of, receiver = mixed[0:count // 2 * 2:2], mixed[1:count // 2 * 2:2]
    margin = jnp.minimum(sizes[source_of] - 1, limit - sizes[receiver]) // 2
    margin = jnp.where((source_of == sequence[0]) | (receiver == sequence[0]) | (sizes[receiver] == 0), 0, jnp.maximum(margin, 0))
    shifted = jax.random.randint(jax.random.fold_in(own, 4), (count // 2,), 0, 1 << 20) % (margin + 1)
    sizes = sizes.at[source_of].add(-shifted).at[receiver].add(shifted)
    members = jnp.searchsorted(jnp.cumsum(sizes), jnp.arange(rows * top), side="right").astype(jnp.int32)
    table = members.reshape(top, rows).T
    table = table[jax.random.permutation(jax.random.fold_in(own, 1), rows)]
    offset_by = jax.random.randint(jax.random.fold_in(own, 2), (rows, 1), 0, top)
    return jnp.take_along_axis(table, (jnp.arange(top)[None, :] + offset_by) % top, axis=1)


def load_shares(amount, total, most, slope, full):
    portions = [(1 << 20) // math.isqrt(grade ** slope) + 1 for grade in range(1, amount + 1)]
    largest = most if full else min(most, max(-(-total // amount), total * portions[0] // sum(portions)))
    least = 1 if total - largest >= amount - 1 else 0
    counts, surplus = [largest] + [least] * (amount - 1), total - largest - least * (amount - 1)
    while surplus > 0:
        free = [i for i in range(1, amount) if counts[i] < largest] or [i for i in range(1, amount) if counts[i] < most]
        mass, left = sum([portions[i] for i in free]), surplus
        for i in free:
            extra = min(most - counts[i], max(1, left * portions[i] // mass), surplus)
            counts[i] = counts[i] + extra
            surplus = surplus - extra
    return np.array(counts)


def normal_values(own_key, extent, deviation, limit, pieces=(), held_as=jnp.bfloat16):
    gain = levels(own_key, extent, pieces, -0.22, 0.18) if pieces else 1.0
    values = jax.random.normal(own_key, extent, jnp.float32) * deviation * gain
    return jnp.minimum(jnp.maximum(values, -limit), limit).astype(held_as)


def heavy_noise(own_key, shape, spread, most, shards, heavy, held_as=jnp.bfloat16):
    values = spread * jax.random.normal(own_key, shape, jnp.float32)
    if shards:
        values = values * levels(own_key, shape, shards, -0.22, 0.18)
    return jnp.clip(strengthened(values, jax.random.fold_in(own_key, 3), *heavy), -most, most).astype(held_as)


def setup_inputs(seed: int = 0) -> dict:
    splits = jax.random.split(jax.random.key(seed), 15)
    queries = draw_queries(jax.random.fold_in(splits[14], 71), 0)
    new_keys = draw_new_keys(jax.random.fold_in(splits[14], 71), 0)
    new_values = normal_values(splits[2], (R, KVH * HD), 1.0, 5.0, ((0, 128),))
    key_cache = draw_key_cache(jax.random.fold_in(splits[14], 71), 0)
    value_cache = normal_values(splits[4], (R, CACHE, KVH * HD), 1.0, 5.0, ((0, 128),))
    lengths = ragged_sizes(splits[5], R, R * CACHE // 4, CACHE, 2).astype(jnp.int32)
    residual = draw_residual(jax.random.fold_in(splits[14], 71), 0)
    out_weight = normal_values(splits[7], (D, D), (D // 4) ** -0.5, 0.1875, ((1, 16),))
    norm_gain = jnp.clip(1.0 + 0.15 * jax.random.normal(splits[8], (D,), jnp.float32), 0.25, 1.75)
    router = normal_values(splits[9], (D, EXPERTS), D ** -0.5, 0.09375, ((0, 16),), jnp.float32)
    gate_weight = normal_values(splits[10], (EXPERTS, D, FF), D ** -0.5, 0.09375, ((0, 8), (2, 16)))
    up_weight = normal_values(splits[11], (EXPERTS, D, FF), D ** -0.5, 0.09375, ((0, 8), (2, 16)))
    down_weight = heavy_noise(splits[12], (EXPERTS, FF, D), FF ** -0.5, 0.09375, ((0, 8), (1, 16)), (1, 2, 16, 2.0))
    routes_keys = jax.random.split(jax.random.fold_in(splits[13], 1), R // RROW)
    routes_turns = jax.random.permutation(jax.random.fold_in(splits[13], 3), R // RROW)
    routes = jax.vmap(lambda own, number: shared_out(jax.random.fold_in(splits[13], 2), own, number, RROW, EXPERTS, 2, CAP, 2))(routes_keys, routes_turns).reshape((R, 2))
    return {"queries": queries, "new_keys": new_keys, "new_values": new_values, "key_cache": key_cache, "value_cache": value_cache, "lengths": lengths, "residual": residual, "out_weight": out_weight, "norm_gain": norm_gain, "router": router, "gate_weight": gate_weight, "up_weight": up_weight, "down_weight": down_weight, "routes": routes}


EPSILON = 1e-05
FLOOR = -1e+30

def attend_request(operands):
    query_row, key_new, value_new, key_rows, value_rows, length = operands
    group_size = QH // KVH
    score_scale = 1.0 / math.sqrt(HD)
    queries_f = query_row.reshape(KVH, group_size, HD).astype(jnp.float32)
    keys_f = key_rows.reshape(CACHE, KVH, HD).astype(jnp.float32)
    values_f = value_rows.reshape(CACHE, KVH, HD).astype(jnp.float32)
    scores = jnp.einsum('kgd,pkd->kgp', queries_f, keys_f) * score_scale
    score_new = jnp.einsum('kgd,kd->kg', queries_f, key_new.reshape(KVH, HD).astype(jnp.float32)) * score_scale
    live_mask = (jnp.arange(CACHE, dtype=jnp.int32) < length)[None, None, :]
    masked = jnp.where(live_mask, scores, FLOOR)
    largest = jnp.maximum(lax.optimization_barrier(jnp.max(masked, axis=-1)), score_new)
    weights = jnp.where(live_mask, jnp.exp(masked - largest[..., None]), 0.0)
    weight_new = jnp.exp(score_new - largest)
    denoms = lax.optimization_barrier(jnp.sum(weights, axis=-1)) + weight_new
    rounded = lax.optimization_barrier(weights.astype(jnp.bfloat16)).astype(jnp.float32)
    rounded_new = lax.optimization_barrier(weight_new.astype(jnp.bfloat16)).astype(jnp.float32)
    totals = jnp.einsum('kgp,pkd->kgd', rounded, values_f)
    totals = totals + rounded_new[..., None] * value_new.reshape(KVH, 1, HD).astype(jnp.float32)
    return (totals / denoms[..., None]).reshape(QH * HD).astype(jnp.bfloat16)

def reference(queries, new_keys, new_values, key_cache, value_cache, lengths, residual, out_weight, norm_gain, router, gate_weight, up_weight, down_weight, routes):
    attended = lax.map(attend_request, (queries, new_keys, new_values, key_cache, value_cache, lengths))
    hidden = residual.astype(jnp.float32) + jnp.dot(attended, out_weight, preferred_element_type=jnp.float32)
    mean_square = lax.optimization_barrier(jnp.sum(hidden * hidden, axis=-1, keepdims=True)) / D
    inverse = lax.rsqrt(mean_square + EPSILON)
    scaled = hidden * norm_gain
    logits = jnp.dot(scaled, router, precision=lax.Precision.HIGHEST) * inverse
    normed = (scaled * inverse).astype(jnp.bfloat16)
    picked = jnp.take_along_axis(logits, routes, axis=1)
    first_weight = jax.nn.sigmoid(picked[:, 0] - picked[:, 1])
    second_weight = 1.0 - first_weight

    def one_expert(mixed, expert_index):
        gate_sum = jnp.dot(normed, gate_weight[expert_index], preferred_element_type=jnp.float32)
        up_sum = jnp.dot(normed, up_weight[expert_index], preferred_element_type=jnp.float32)
        inner = (jax.nn.silu(gate_sum) * up_sum).astype(jnp.bfloat16)
        output = jnp.dot(inner, down_weight[expert_index], preferred_element_type=jnp.float32).astype(jnp.bfloat16)
        output = lax.optimization_barrier(output).astype(jnp.float32)
        factor = jnp.where(routes[:, 0] == expert_index, first_weight, 0.0) + jnp.where(routes[:, 1] == expert_index, second_weight, 0.0)
        return (mixed + factor[:, None] * output, None)
    mixed, _ = lax.scan(one_expert, jnp.zeros(hidden.shape, jnp.float32), jnp.arange(EXPERTS, dtype=jnp.int32))
    return (hidden + mixed).astype(jnp.bfloat16)
```

```python
import math

import jax
import jax.numpy as jnp
from jax import lax
from jax.sharding import PartitionSpec as P

D = 4096
QH = 32
KVH = 8
HD = 128
CACHE = 512


EPSILON = 1e-05
FLOOR = -1e30


def attend_local(queries, new_keys, new_values, key_cache, value_cache, lengths):
    request_count = queries.shape[0]
    group_size = QH // KVH
    score_scale = 1.0 / math.sqrt(HD)
    block_size = math.gcd(CACHE, 256)
    query_heads = queries.reshape(request_count, KVH, group_size, HD)
    key_view = key_cache.reshape(request_count, CACHE, KVH, HD)
    value_view = value_cache.reshape(request_count, CACHE, KVH, HD)
    score_new = (
        jnp.einsum(
            "rkgd,rkd->rkg",
            query_heads,
            new_keys.reshape(request_count, KVH, HD),
            preferred_element_type=jnp.float32,
        )
        * score_scale
    )
    value_start = jnp.broadcast_to(
        new_values.reshape(request_count, KVH, 1, HD).astype(jnp.float32),
        (request_count, KVH, group_size, HD),
    )
    initial = (score_new, jnp.ones_like(score_new), value_start)

    def block_step(block_index, carried):
        running_max, running_den, running_tot = carried
        offset = block_index * block_size
        keys_part = lax.dynamic_slice_in_dim(key_view, offset, block_size, 1)
        values_part = lax.dynamic_slice_in_dim(value_view, offset, block_size, 1)
        scores = (
            jnp.einsum(
                "rkgd,rpkd->rkgp", query_heads, keys_part, preferred_element_type=jnp.float32
            )
            * score_scale
        )
        positions = offset + jnp.arange(block_size, dtype=jnp.int32)
        live_mask = (positions[None, :] < lengths[:, None])[:, None, None, :]
        masked = jnp.where(live_mask, scores, FLOOR)
        new_max = jnp.maximum(running_max, jnp.max(masked, axis=-1))
        weights = jnp.where(live_mask, jnp.exp(masked - new_max[..., None]), 0.0)
        shrink = jnp.exp(running_max - new_max)
        new_den = running_den * shrink + jnp.sum(weights, axis=-1)
        new_tot = running_tot * shrink[..., None] + jnp.einsum(
            "rkgp,rpkd->rkgd",
            weights.astype(jnp.bfloat16),
            values_part,
            preferred_element_type=jnp.float32,
        )
        return (new_max, new_den, new_tot)

    block_total = (jnp.max(lengths) + block_size - 1) // block_size
    final_max, final_den, final_tot = lax.fori_loop(0, block_total, block_step, initial)
    return (final_tot / final_den[..., None]).astype(jnp.bfloat16).reshape(request_count, QH * HD)


def local(
    queries,
    new_keys,
    new_values,
    key_cache,
    value_cache,
    lengths,
    residual,
    out_weight,
    norm_gain,
    router,
    gate_weight,
    up_weight,
    down_weight,
    routes,
):
    attended = attend_local(queries, new_keys, new_values, key_cache, value_cache, lengths)
    hidden = residual.astype(jnp.float32) + jnp.dot(
        lax.all_gather(attended, "ffn", axis=0, tiled=True),
        out_weight,
        preferred_element_type=jnp.float32,
    )
    scaled = hidden * norm_gain
    square_part = jnp.sum(hidden * hidden, axis=-1, keepdims=True)
    logit_part = jnp.dot(scaled, router, precision=lax.Precision.HIGHEST)
    stats = lax.psum(jnp.concatenate([square_part, logit_part], axis=1), "ffn")
    inverse = lax.rsqrt(stats[:, :1] / D + EPSILON)
    logits = stats[:, 1:] * inverse
    normed = (scaled * inverse).astype(jnp.bfloat16)
    expert_count = lax.axis_size("expert")
    row_count = routes.shape[0]
    capacity = row_count // 2
    expert_ids = jnp.arange(expert_count, dtype=jnp.int32)
    chosen = routes[:, :, None] == expert_ids[None, None, :]
    picked = jnp.sum(jnp.where(chosen, logits[:, None, :], 0.0), axis=-1)
    first_weight = jax.nn.sigmoid(picked[:, 0] - picked[:, 1])
    route_weights = jnp.stack([first_weight, 1.0 - first_weight], axis=1)
    flat_hits = chosen.astype(jnp.int32).reshape(row_count * 2, expert_count)
    earlier = jnp.cumsum(flat_hits, axis=0) - flat_hits
    slots = jnp.sum(earlier * flat_hits, axis=-1).reshape(row_count, 2)
    targets = routes * capacity + slots
    slot_ids = jnp.arange(expert_count * capacity, dtype=jnp.int32)
    slot_hits = slot_ids[:, None, None] == targets[None, :, :]
    dispatch = jnp.sum(slot_hits.astype(jnp.float32), axis=-1).astype(jnp.bfloat16)
    combine = jnp.sum(jnp.where(slot_hits, route_weights[None, :, :], 0.0), axis=-1).T
    gate_local = gate_weight[0]
    up_local = up_weight[0]
    down_local = down_weight[0]
    share_rows = (
        jnp.dot(dispatch, normed, preferred_element_type=jnp.float32)
        .astype(jnp.bfloat16)
        .reshape(expert_count, capacity, normed.shape[1])
    )
    feature_blocks = lax.axis_size("ffn")
    received = lax.all_to_all(share_rows, "expert", split_axis=0, concat_axis=0, tiled=True)
    part_rows = lax.all_gather(
        received.reshape(expert_count * capacity, normed.shape[1]), "ffn", axis=0, tiled=False
    )
    part_rows = part_rows.transpose(1, 0, 2).reshape(expert_count * capacity, -1)
    gate_next = jnp.dot(part_rows, gate_local, preferred_element_type=jnp.float32)
    up_next = jnp.dot(part_rows, up_local, preferred_element_type=jnp.float32)
    inner = (jax.nn.silu(gate_next) * up_next).astype(jnp.bfloat16)
    partial_out = jnp.dot(inner, down_local, preferred_element_type=jnp.float32)
    partial_out = partial_out.reshape(-1, feature_blocks, normed.shape[1]).transpose(1, 0, 2)
    summed = lax.psum_scatter(
        partial_out.astype(jnp.bfloat16), "ffn", scatter_dimension=0, tiled=True
    ).reshape(expert_count, capacity, normed.shape[1])
    returned = lax.all_to_all(summed, "expert", split_axis=0, concat_axis=0, tiled=True)
    mixed = jnp.dot(
        combine,
        returned.reshape(expert_count * capacity, -1).astype(jnp.float32),
        precision=lax.Precision.HIGHEST,
    )
    return (hidden + mixed).astype(jnp.bfloat16)


def solution(mesh):
    placed = (
        P(("expert", "ffn"), None),
        P(("expert", "ffn"), None),
        P(("expert", "ffn"), None),
        P(("expert", "ffn"), None, None),
        P(("expert", "ffn"), None, None),
        P(("expert", "ffn")),
        P("expert", "ffn"),
        P(None, "ffn"),
        P("ffn"),
        P("ffn", None),
        P("expert", None, "ffn"),
        P("expert", None, "ffn"),
        P("expert", "ffn", None),
        P("expert", None),
    )
    return jax.shard_map(
        local, mesh=mesh, in_specs=placed, out_specs=P("expert", "ffn"), check_vma=False
    )
```

```python
import math

import jax
import jax.numpy as jnp
from jax import lax
from jax.sharding import PartitionSpec as P

D = 4096
QH = 32
KVH = 8
HD = 128
CACHE = 512


EPSILON = 1e-05
FLOOR = -1e30


def butterfly_sum(value, axis_name):
    size = lax.axis_size(axis_name)
    step = 1
    while step < size:
        pairs = [(j, j ^ step) for j in range(size)]
        value = value + lax.ppermute(value, axis_name, pairs)
        step *= 2
    return value


def gather_by_exchange(value, axis_name):
    size = lax.axis_size(axis_name)
    copies = jnp.broadcast_to(value[None], (size,) + value.shape)
    return lax.all_to_all(copies, axis_name, 0, 0, tiled=True)


def attend_local(queries, new_keys, new_values, key_cache, value_cache, lengths):
    request_count = queries.shape[0]
    group_size = QH // KVH
    score_scale = 1.0 / math.sqrt(HD)
    block_size = math.gcd(CACHE, 256)
    query_heads = queries.reshape(request_count, KVH, group_size, HD)
    key_view = key_cache.reshape(request_count, CACHE, KVH, HD)
    value_view = value_cache.reshape(request_count, CACHE, KVH, HD)
    score_new = (
        jnp.einsum(
            "rkgd,rkd->rkg",
            query_heads,
            new_keys.reshape(request_count, KVH, HD),
            preferred_element_type=jnp.float32,
        )
        * score_scale
    )
    value_start = jnp.broadcast_to(
        new_values.reshape(request_count, KVH, 1, HD).astype(jnp.float32),
        (request_count, KVH, group_size, HD),
    )
    initial = (score_new, jnp.ones_like(score_new), value_start)

    def block_step(block_index, carried):
        running_max, running_den, running_tot = carried
        offset = block_index * block_size
        keys_part = lax.dynamic_slice_in_dim(key_view, offset, block_size, 1)
        values_part = lax.dynamic_slice_in_dim(value_view, offset, block_size, 1)
        scores = (
            jnp.einsum(
                "rkgd,rpkd->rkgp", query_heads, keys_part, preferred_element_type=jnp.float32
            )
            * score_scale
        )
        positions = offset + jnp.arange(block_size, dtype=jnp.int32)
        live_mask = (positions[None, :] < lengths[:, None])[:, None, None, :]
        masked = jnp.where(live_mask, scores, FLOOR)
        new_max = jnp.maximum(running_max, jnp.max(masked, axis=-1))
        weights = jnp.where(live_mask, jnp.exp(masked - new_max[..., None]), 0.0)
        shrink = jnp.exp(running_max - new_max)
        new_den = running_den * shrink + jnp.sum(weights, axis=-1)
        new_tot = running_tot * shrink[..., None] + jnp.einsum(
            "rkgp,rpkd->rkgd",
            weights.astype(jnp.bfloat16),
            values_part,
            preferred_element_type=jnp.float32,
        )
        return (new_max, new_den, new_tot)

    block_total = (jnp.max(lengths) + block_size - 1) // block_size
    final_max, final_den, final_tot = lax.fori_loop(0, block_total, block_step, initial)
    return (final_tot / final_den[..., None]).astype(jnp.bfloat16).reshape(request_count, QH * HD)


def local(
    queries,
    new_keys,
    new_values,
    key_cache,
    value_cache,
    lengths,
    residual,
    out_weight,
    norm_gain,
    router,
    gate_weight,
    up_weight,
    down_weight,
    routes,
):
    attended = attend_local(queries, new_keys, new_values, key_cache, value_cache, lengths)
    gathered = gather_by_exchange(attended, "ffn").reshape(-1, attended.shape[1])
    hidden = residual.astype(jnp.float32) + jnp.dot(
        gathered,
        out_weight,
        preferred_element_type=jnp.float32,
    )
    scaled = hidden * norm_gain
    square_part = jnp.sum(hidden * hidden, axis=-1, keepdims=True)
    logit_part = jnp.dot(scaled, router, precision=lax.Precision.HIGHEST)
    stats = butterfly_sum(jnp.concatenate([square_part, logit_part], axis=1), "ffn")
    inverse = lax.rsqrt(stats[:, :1] / D + EPSILON)
    logits = stats[:, 1:] * inverse
    normed = (scaled * inverse).astype(jnp.bfloat16)
    expert_count = lax.axis_size("expert")
    row_count = routes.shape[0]
    capacity = row_count // 2
    expert_ids = jnp.arange(expert_count, dtype=jnp.int32)
    chosen = routes[:, :, None] == expert_ids[None, None, :]
    picked = jnp.sum(jnp.where(chosen, logits[:, None, :], 0.0), axis=-1)
    first_weight = jax.nn.sigmoid(picked[:, 0] - picked[:, 1])
    route_weights = jnp.stack([first_weight, 1.0 - first_weight], axis=1)
    flat_hits = chosen.astype(jnp.int32).reshape(row_count * 2, expert_count)
    earlier = jnp.cumsum(flat_hits, axis=0) - flat_hits
    slots = jnp.sum(earlier * flat_hits, axis=-1).reshape(row_count, 2)
    targets = routes * capacity + slots
    slot_ids = jnp.arange(expert_count * capacity, dtype=jnp.int32)
    slot_hits = slot_ids[:, None, None] == targets[None, :, :]
    dispatch = jnp.sum(slot_hits.astype(jnp.float32), axis=-1).astype(jnp.bfloat16)
    combine = jnp.sum(jnp.where(slot_hits, route_weights[None, :, :], 0.0), axis=-1).T
    gate_local = gate_weight[0]
    up_local = up_weight[0]
    down_local = down_weight[0]
    share_rows = (
        jnp.dot(dispatch, normed, preferred_element_type=jnp.float32)
        .astype(jnp.bfloat16)
        .reshape(expert_count, capacity, normed.shape[1])
    )
    feature_blocks = lax.axis_size("ffn")
    received = lax.all_to_all(share_rows, "expert", split_axis=0, concat_axis=0, tiled=True)
    part_rows = gather_by_exchange(
        received.reshape(expert_count * capacity, normed.shape[1]), "ffn"
    )
    part_rows = part_rows.transpose(1, 0, 2).reshape(expert_count * capacity, -1)
    gate_next = jnp.dot(part_rows, gate_local, preferred_element_type=jnp.float32)
    up_next = jnp.dot(part_rows, up_local, preferred_element_type=jnp.float32)
    inner = (jax.nn.silu(gate_next) * up_next).astype(jnp.bfloat16)
    partial_out = jnp.dot(inner, down_local, preferred_element_type=jnp.float32)
    partial_out = partial_out.reshape(-1, feature_blocks, normed.shape[1]).transpose(1, 0, 2)
    pieces = lax.all_to_all(partial_out.astype(jnp.bfloat16), "ffn", 0, 0, tiled=True)
    summed = (
        jnp.sum(pieces.astype(jnp.float32), axis=0)
        .astype(jnp.bfloat16)
        .reshape(expert_count, capacity, normed.shape[1])
    )
    returned = lax.all_to_all(summed, "expert", split_axis=0, concat_axis=0, tiled=True)
    mixed = jnp.dot(
        combine,
        returned.reshape(expert_count * capacity, -1).astype(jnp.float32),
        precision=lax.Precision.HIGHEST,
    )
    return (hidden + mixed).astype(jnp.bfloat16)


def solution(mesh):
    placed = (
        P(("expert", "ffn"), None),
        P(("expert", "ffn"), None),
        P(("expert", "ffn"), None),
        P(("expert", "ffn"), None, None),
        P(("expert", "ffn"), None, None),
        P(("expert", "ffn")),
        P("expert", "ffn"),
        P(None, "ffn"),
        P("ffn"),
        P("ffn", None),
        P("expert", None, "ffn"),
        P("expert", None, "ffn"),
        P("expert", "ffn", None),
        P("expert", None),
    )
    return jax.shard_map(
        local, mesh=mesh, in_specs=placed, out_specs=P("expert", "ffn"), check_vma=False
    )
```

```python
import math

import jax
import jax.numpy as jnp
from jax import lax
from jax.sharding import PartitionSpec as P

D = 4096
QH = 32
KVH = 8
HD = 128
CACHE = 512


EPSILON = 1e-05
FLOOR = -1e30


def butterfly_sum(value, axis_name):
    size = lax.axis_size(axis_name)
    step = 1
    while step < size:
        pairs = [(j, j ^ step) for j in range(size)]
        value = value + lax.ppermute(value, axis_name, pairs)
        step *= 2
    return value


def gather_by_exchange(value, axis_name):
    size = lax.axis_size(axis_name)
    copies = jnp.broadcast_to(value[None], (size,) + value.shape)
    return lax.all_to_all(copies, axis_name, 0, 0, tiled=True)


def attend_local(queries, new_keys, new_values, key_cache, value_cache, lengths):
    request_count = queries.shape[0]
    group_size = QH // KVH
    score_scale = 1.0 / math.sqrt(HD)
    query_heads = queries.reshape(request_count, KVH, group_size, HD)
    head_eye = jnp.eye(KVH, dtype=queries.dtype)[None, :, None, :, None]
    spread_queries = (query_heads[:, :, :, None, :] * head_eye).reshape(request_count, QH, KVH * HD)
    scores = (
        jnp.einsum("rhc,rpc->rhp", spread_queries, key_cache, preferred_element_type=jnp.float32)
        * score_scale
    )
    score_new = (
        jnp.einsum(
            "rkgd,rkd->rkg",
            query_heads,
            new_keys.reshape(request_count, KVH, HD),
            preferred_element_type=jnp.float32,
        )
        * score_scale
    ).reshape(request_count, QH)
    positions = jnp.arange(key_cache.shape[1], dtype=jnp.int32)
    live_mask = (positions[None, :] < lengths[:, None])[:, None, :]
    masked = jnp.where(live_mask, scores, FLOOR)
    largest = jnp.maximum(jnp.max(masked, axis=-1), score_new)
    weights = jnp.where(live_mask, jnp.exp(masked - largest[..., None]), 0.0)
    weight_new = jnp.exp(score_new - largest)
    denoms = jnp.sum(weights, axis=-1) + weight_new
    spread_totals = jnp.einsum(
        "rhp,rpc->rhc", weights.astype(jnp.bfloat16), value_cache, preferred_element_type=jnp.float32
    ).reshape(request_count, KVH, group_size, KVH, HD)
    totals = jnp.sum(spread_totals * head_eye.astype(jnp.float32), axis=3)
    rounded_new = weight_new.astype(jnp.bfloat16).astype(jnp.float32).reshape(request_count, KVH, group_size)
    totals = totals + rounded_new[..., None] * new_values.reshape(request_count, KVH, 1, HD).astype(jnp.float32)
    denoms = denoms.reshape(request_count, KVH, group_size)
    return (totals / denoms[..., None]).astype(jnp.bfloat16).reshape(request_count, QH * HD)


def local(
    queries,
    new_keys,
    new_values,
    key_cache,
    value_cache,
    lengths,
    residual,
    out_weight,
    norm_gain,
    router,
    gate_weight,
    up_weight,
    down_weight,
    routes,
):
    attended = attend_local(queries, new_keys, new_values, key_cache, value_cache, lengths)
    gathered = gather_by_exchange(attended, "ffn").reshape(-1, attended.shape[1])
    hidden = residual.astype(jnp.float32) + jnp.dot(
        gathered,
        out_weight,
        preferred_element_type=jnp.float32,
    )
    scaled = hidden * norm_gain
    square_part = jnp.sum(hidden * hidden, axis=-1, keepdims=True)
    logit_part = jnp.dot(scaled, router, precision=lax.Precision.HIGHEST)
    stats = butterfly_sum(jnp.concatenate([square_part, logit_part], axis=1), "ffn")
    inverse = lax.rsqrt(stats[:, :1] / D + EPSILON)
    logits = stats[:, 1:] * inverse
    normed = (scaled * inverse).astype(jnp.bfloat16)
    expert_count = lax.axis_size("expert")
    row_count = routes.shape[0]
    capacity = row_count // 2
    expert_ids = jnp.arange(expert_count, dtype=jnp.int32)
    chosen = routes[:, :, None] == expert_ids[None, None, :]
    picked = jnp.sum(jnp.where(chosen, logits[:, None, :], 0.0), axis=-1)
    first_weight = jax.nn.sigmoid(picked[:, 0] - picked[:, 1])
    route_weights = jnp.stack([first_weight, 1.0 - first_weight], axis=1)
    flat_hits = chosen.astype(jnp.int32).reshape(row_count * 2, expert_count)
    earlier = jnp.cumsum(flat_hits, axis=0) - flat_hits
    slots = jnp.sum(earlier * flat_hits, axis=-1).reshape(row_count, 2)
    targets = routes * capacity + slots
    slot_ids = jnp.arange(expert_count * capacity, dtype=jnp.int32)
    slot_hits = slot_ids[:, None, None] == targets[None, :, :]
    dispatch = jnp.sum(slot_hits.astype(jnp.float32), axis=-1).astype(jnp.bfloat16)
    combine = jnp.sum(jnp.where(slot_hits, route_weights[None, :, :], 0.0), axis=-1).T
    gate_local = gate_weight[0]
    up_local = up_weight[0]
    down_local = down_weight[0]
    share_rows = (
        jnp.dot(dispatch, normed, preferred_element_type=jnp.float32)
        .astype(jnp.bfloat16)
        .reshape(expert_count, capacity, normed.shape[1])
    )
    feature_blocks = lax.axis_size("ffn")
    width = normed.shape[1]
    outgoing = jnp.broadcast_to(
        share_rows[:, None], (expert_count, feature_blocks, capacity, width)
    ).reshape(expert_count * feature_blocks, capacity, width)
    incoming = lax.all_to_all(outgoing, ("expert", "ffn"), 0, 0, tiled=True)
    part_rows = (
        incoming.reshape(expert_count, feature_blocks, capacity, width)
        .transpose(0, 2, 1, 3)
        .reshape(expert_count * capacity, feature_blocks * width)
    )
    gate_next = jnp.dot(part_rows, gate_local, preferred_element_type=jnp.float32)
    up_next = jnp.dot(part_rows, up_local, preferred_element_type=jnp.float32)
    inner = (jax.nn.silu(gate_next) * up_next).astype(jnp.bfloat16)
    partial_out = jnp.dot(inner, down_local, preferred_element_type=jnp.float32)
    partial_out = (
        partial_out.reshape(expert_count, capacity, feature_blocks, width)
        .transpose(0, 2, 1, 3)
        .reshape(expert_count * feature_blocks, capacity, width)
    )
    pieces = lax.all_to_all(partial_out.astype(jnp.bfloat16), ("expert", "ffn"), 0, 0, tiled=True)
    returned = (
        jnp.sum(pieces.reshape(expert_count, feature_blocks, capacity, width).astype(jnp.float32), axis=1)
        .astype(jnp.bfloat16)
    )
    mixed = jnp.dot(
        combine,
        returned.reshape(expert_count * capacity, -1).astype(jnp.float32),
        precision=lax.Precision.HIGHEST,
    )
    return (hidden + mixed).astype(jnp.bfloat16)


def solution(mesh):
    placed = (
        P(("expert", "ffn"), None),
        P(("expert", "ffn"), None),
        P(("expert", "ffn"), None),
        P(("expert", "ffn"), None, None),
        P(("expert", "ffn"), None, None),
        P(("expert", "ffn")),
        P("expert", "ffn"),
        P(None, "ffn"),
        P("ffn"),
        P("ffn", None),
        P("expert", None, "ffn"),
        P("expert", None, "ffn"),
        P("expert", "ffn", None),
        P("expert", None),
    )
    return jax.shard_map(
        local, mesh=mesh, in_specs=placed, out_specs=P("expert", "ffn"), check_vma=False
    )
```

```python
import math

import jax
import jax.numpy as jnp
from jax import lax
from jax.sharding import PartitionSpec as P


D = 4096
QH = 32
KVH = 8
HD = 128


EPSILON = 1e-05
FLOOR = -1e30


def butterfly_sum(value, axis_name):
    size = lax.axis_size(axis_name)
    step = 1
    while step < size:
        pairs = [(j, j ^ step) for j in range(size)]
        value = value + lax.ppermute(value, axis_name, pairs)
        step *= 2
    return value


def gather_by_exchange(value, axis_name):
    size = lax.axis_size(axis_name)
    copies = jnp.broadcast_to(value[None], (size,) + value.shape)
    return lax.all_to_all(copies, axis_name, 0, 0, tiled=True)


def attend_local(queries, new_keys, new_values, key_cache, value_cache, lengths):
    request_count = queries.shape[0]
    group_size = QH // KVH
    score_scale = 1.0 / math.sqrt(HD)
    query_heads = queries.reshape(request_count, KVH, group_size, HD)
    head_eye = jnp.eye(KVH, dtype=queries.dtype)[None, :, None, :, None]
    spread_queries = (query_heads[:, :, :, None, :] * head_eye).reshape(request_count, QH, KVH * HD)
    scores = (
        jnp.einsum("rhc,rpc->rhp", spread_queries, key_cache, preferred_element_type=jnp.float32)
        * score_scale
    )
    score_new = (
        jnp.einsum(
            "rkgd,rkd->rkg",
            query_heads,
            new_keys.reshape(request_count, KVH, HD),
            preferred_element_type=jnp.float32,
        )
        * score_scale
    ).reshape(request_count, QH)
    positions = jnp.arange(key_cache.shape[1], dtype=jnp.int32)
    live_mask = (positions[None, :] < lengths[:, None])[:, None, :]
    masked = jnp.where(live_mask, scores, FLOOR)
    largest = jnp.maximum(jnp.max(masked, axis=-1), score_new)
    weights = jnp.where(live_mask, jnp.exp(masked - largest[..., None]), 0.0)
    weight_new = jnp.exp(score_new - largest)
    denoms = jnp.sum(weights, axis=-1) + weight_new
    spread_totals = jnp.einsum(
        "rhp,rpc->rhc", weights.astype(jnp.bfloat16), value_cache, preferred_element_type=jnp.float32
    ).reshape(request_count, KVH, group_size, KVH, HD)
    totals = jnp.sum(spread_totals * head_eye.astype(jnp.float32), axis=3)
    rounded_new = weight_new.astype(jnp.bfloat16).astype(jnp.float32).reshape(request_count, KVH, group_size)
    totals = totals + rounded_new[..., None] * new_values.reshape(request_count, KVH, 1, HD).astype(jnp.float32)
    denoms = denoms.reshape(request_count, KVH, group_size)
    return (totals / denoms[..., None]).astype(jnp.bfloat16).reshape(request_count, QH * HD)


def local(
    queries,
    new_keys,
    new_values,
    key_cache,
    value_cache,
    lengths,
    residual,
    out_weight,
    norm_gain,
    router,
    gate_weight,
    up_weight,
    down_weight,
    routes,
):
    attended = attend_local(queries, new_keys, new_values, key_cache, value_cache, lengths)
    gain_high = norm_gain.astype(jnp.bfloat16)
    gain_low = (norm_gain - gain_high.astype(jnp.float32)).astype(jnp.bfloat16)
    gain_width = norm_gain.shape[0]
    gain_row = jnp.concatenate(
        [gain_high, gain_low, jnp.zeros((attended.shape[1] - 2 * gain_width,), jnp.bfloat16)]
    )[None]
    exchanged = gather_by_exchange(jnp.concatenate([attended, gain_row], axis=0), "ffn")
    gathered = exchanged[:, :-1].reshape(-1, attended.shape[1])
    gain_parts = exchanged[:, -1, : 2 * gain_width].reshape(-1, 2, gain_width).astype(jnp.float32)
    gain_full = (gain_parts[:, 0] + gain_parts[:, 1]).reshape(-1)
    hidden = residual.astype(jnp.float32) + jnp.dot(
        gathered,
        out_weight,
        preferred_element_type=jnp.float32,
    )
    scaled = hidden * norm_gain
    square_part = jnp.sum(hidden * hidden, axis=-1, keepdims=True)
    logit_part = jnp.dot(scaled, router, precision=lax.Precision.HIGHEST)
    stats = butterfly_sum(jnp.concatenate([square_part, logit_part], axis=1), "ffn")
    inverse = lax.rsqrt(stats[:, :1] / D + EPSILON)
    logits = stats[:, 1:] * inverse
    scaled_rows = scaled.astype(jnp.bfloat16)
    expert_count = lax.axis_size("expert")
    row_count = routes.shape[0]
    capacity = row_count // 2
    expert_ids = jnp.arange(expert_count, dtype=jnp.int32)
    chosen = routes[:, :, None] == expert_ids[None, None, :]
    picked = jnp.sum(jnp.where(chosen, logits[:, None, :], 0.0), axis=-1)
    first_weight = jax.nn.sigmoid(picked[:, 0] - picked[:, 1])
    route_weights = jnp.stack([first_weight, 1.0 - first_weight], axis=1)
    flat_hits = chosen.astype(jnp.int32).reshape(row_count * 2, expert_count)
    earlier = jnp.cumsum(flat_hits, axis=0) - flat_hits
    slots = jnp.sum(earlier * flat_hits, axis=-1).reshape(row_count, 2)
    targets = routes * capacity + slots
    slot_ids = jnp.arange(expert_count * capacity, dtype=jnp.int32)
    slot_hits = slot_ids[:, None, None] == targets[None, :, :]
    dispatch = jnp.sum(slot_hits.astype(jnp.float32), axis=-1).astype(jnp.bfloat16)
    dispatch, targets = lax.optimization_barrier((dispatch, targets))
    slot_hits = slot_ids[:, None, None] == targets[None, :, :]
    combine = jnp.sum(jnp.where(slot_hits, route_weights[None, :, :], 0.0), axis=-1).T
    gate_local = gate_weight[0]
    up_local = up_weight[0]
    down_local = down_weight[0]
    share_rows = (
        jnp.dot(dispatch, scaled_rows, preferred_element_type=jnp.float32)
        .astype(jnp.bfloat16)
        .reshape(expert_count, capacity, scaled_rows.shape[1])
    )
    feature_blocks = lax.axis_size("ffn")
    width = scaled_rows.shape[1]
    outgoing = jnp.broadcast_to(
        share_rows[:, None], (expert_count, feature_blocks, capacity, width)
    ).reshape(expert_count * feature_blocks, capacity, width)
    incoming = lax.all_to_all(outgoing, ("expert", "ffn"), 0, 0, tiled=True)
    part_rows = (
        incoming.reshape(expert_count, feature_blocks, capacity, width)
        .transpose(0, 2, 1, 3)
        .reshape(expert_count * capacity, feature_blocks * width)
    )
    rows_f = part_rows.astype(jnp.float32)
    rows_hidden = rows_f / gain_full
    row_inverse = lax.rsqrt(jnp.sum(rows_hidden * rows_hidden, axis=-1, keepdims=True) / D + EPSILON)
    normed_rows = (rows_f * row_inverse).astype(jnp.bfloat16)
    gate_next = jnp.dot(normed_rows, gate_local, preferred_element_type=jnp.float32)
    up_next = jnp.dot(normed_rows, up_local, preferred_element_type=jnp.float32)
    inner = (jax.nn.silu(gate_next) * up_next).astype(jnp.bfloat16)
    partial_out = jnp.dot(inner, down_local, preferred_element_type=jnp.float32)
    partial_out = (
        partial_out.reshape(expert_count, capacity, feature_blocks, width)
        .transpose(0, 2, 1, 3)
        .reshape(expert_count * feature_blocks, capacity, width)
    )
    pieces = lax.all_to_all(partial_out.astype(jnp.bfloat16), ("expert", "ffn"), 0, 0, tiled=True)
    returned = (
        jnp.sum(pieces.reshape(expert_count, feature_blocks, capacity, width).astype(jnp.float32), axis=1)
        .astype(jnp.bfloat16)
    )
    mixed = jnp.dot(
        combine,
        returned.reshape(expert_count * capacity, -1).astype(jnp.float32),
        precision=lax.Precision.HIGHEST,
    )
    return (hidden + mixed).astype(jnp.bfloat16)


def solution(mesh):
    placed = (
        P(("expert", "ffn"), None),
        P(("expert", "ffn"), None),
        P(("expert", "ffn"), None),
        P(("expert", "ffn"), None, None),
        P(("expert", "ffn"), None, None),
        P(("expert", "ffn")),
        P("expert", "ffn"),
        P(None, "ffn"),
        P("ffn"),
        P("ffn", None),
        P("expert", None, "ffn"),
        P("expert", None, "ffn"),
        P("expert", "ffn", None),
        P("expert", None),
    )
    return jax.shard_map(local, mesh=mesh, in_specs=placed, out_specs=P("expert", "ffn"), check_vma=False)
```

```python
import math

import jax
import jax.numpy as jnp
from jax import lax
from jax.sharding import PartitionSpec as P

D = 4096
QH = 32
KVH = 8
HD = 128
CACHE = 512


EPSILON = 1e-05
FLOOR = -1e30


def butterfly_sum(value, axis_name):
    size = lax.axis_size(axis_name)
    step = 1
    while step < size:
        pairs = [(j, j ^ step) for j in range(size)]
        value = value + lax.ppermute(value, axis_name, pairs)
        step *= 2
    return value


def gather_by_exchange(value, axis_name):
    size = lax.axis_size(axis_name)
    copies = jnp.broadcast_to(value[None], (size,) + value.shape)
    return lax.all_to_all(copies, axis_name, 0, 0, tiled=True)


def attend_local(queries, new_keys, new_values, key_cache, value_cache, lengths):
    request_count = queries.shape[0]
    group_size = QH // KVH
    score_scale = 1.0 / math.sqrt(HD)
    query_heads = queries.reshape(request_count, KVH, group_size, HD)
    head_eye = jnp.eye(KVH, dtype=queries.dtype)[None, :, None, :, None]
    spread_queries = (query_heads[:, :, :, None, :] * head_eye).reshape(request_count, QH, KVH * HD)
    scores = (
        jnp.einsum("rhc,rpc->rhp", spread_queries, key_cache, preferred_element_type=jnp.float32)
        * score_scale
    )
    score_new = (
        jnp.einsum("rhc,rc->rh", spread_queries, new_keys, preferred_element_type=jnp.float32)
        * score_scale
    )
    positions = jnp.arange(key_cache.shape[1], dtype=jnp.int32)
    live_mask = (positions[None, :] < lengths[:, None])[:, None, :]
    masked = jnp.where(live_mask, scores, FLOOR)
    largest = jnp.maximum(jnp.max(masked, axis=-1), score_new)
    weights = jnp.where(live_mask, jnp.exp(masked - largest[..., None]), 0.0)
    weight_new = jnp.exp(score_new - largest)
    denoms = jnp.sum(weights, axis=-1) + weight_new
    rounded_new = weight_new.astype(jnp.bfloat16).astype(jnp.float32)
    spread_totals = jnp.einsum(
        "rhp,rpc->rhc", weights.astype(jnp.bfloat16), value_cache, preferred_element_type=jnp.float32
    ) + rounded_new[..., None] * new_values[:, None, :].astype(jnp.float32)
    spread_totals = spread_totals / denoms[..., None]
    totals = jnp.sum(
        spread_totals.reshape(request_count, KVH, group_size, KVH, HD) * head_eye.astype(jnp.float32),
        axis=3,
    )
    return totals.astype(jnp.bfloat16).reshape(request_count, QH * HD)


def local(
    queries,
    new_keys,
    new_values,
    key_cache,
    value_cache,
    lengths,
    residual,
    out_weight,
    norm_gain,
    router,
    gate_weight,
    up_weight,
    down_weight,
    routes,
):
    attended = attend_local(queries, new_keys, new_values, key_cache, value_cache, lengths)
    gathered = gather_by_exchange(attended, "ffn").reshape(-1, attended.shape[1])
    hidden = residual.astype(jnp.float32) + jnp.dot(
        gathered,
        out_weight,
        preferred_element_type=jnp.float32,
    )
    scaled = hidden * norm_gain
    square_part = jnp.sum(hidden * hidden, axis=-1, keepdims=True)
    logit_part = jnp.dot(scaled, router, precision=lax.Precision.HIGHEST)
    stats = jnp.sum(
        gather_by_exchange(jnp.concatenate([square_part, logit_part], axis=1), "ffn"), axis=0
    )
    inverse = lax.rsqrt(stats[:, :1] / D + EPSILON)
    logits = stats[:, 1:] * inverse
    normed = (scaled * inverse).astype(jnp.bfloat16)
    expert_count = lax.axis_size("expert")
    row_count = routes.shape[0]
    capacity = row_count // 2
    expert_ids = jnp.arange(expert_count, dtype=jnp.int32)
    chosen = routes[:, :, None] == expert_ids[None, None, :]
    picked = jnp.sum(jnp.where(chosen, logits[:, None, :], 0.0), axis=-1)
    first_weight = jax.nn.sigmoid(picked[:, 0] - picked[:, 1])
    route_weights = jnp.stack([first_weight, 1.0 - first_weight], axis=1)
    flat_hits = chosen.astype(jnp.int32).reshape(row_count * 2, expert_count)
    earlier = jnp.cumsum(flat_hits, axis=0) - flat_hits
    slots = jnp.sum(earlier * flat_hits, axis=-1).reshape(row_count, 2)
    targets = routes * capacity + slots
    slot_ids = jnp.arange(expert_count * capacity, dtype=jnp.int32)
    slot_hits = slot_ids[:, None, None] == targets[None, :, :]
    dispatch = jnp.sum(slot_hits.astype(jnp.float32), axis=-1).astype(jnp.bfloat16)
    combine = jnp.sum(jnp.where(slot_hits, route_weights[None, :, :], 0.0), axis=-1).T
    gate_local = gate_weight[0]
    up_local = up_weight[0]
    down_local = down_weight[0]
    share_rows = (
        jnp.dot(dispatch, normed, preferred_element_type=jnp.float32)
        .astype(jnp.bfloat16)
        .reshape(expert_count, capacity, normed.shape[1])
    )
    feature_blocks = lax.axis_size("ffn")
    width = normed.shape[1]
    outgoing = jnp.broadcast_to(
        share_rows[:, None], (expert_count, feature_blocks, capacity, width)
    ).reshape(expert_count * feature_blocks, capacity, width)
    incoming = lax.all_to_all(outgoing, ("expert", "ffn"), 0, 0, tiled=True)
    part_rows = (
        incoming.reshape(expert_count, feature_blocks, capacity, width)
        .transpose(0, 2, 1, 3)
        .reshape(expert_count * capacity, feature_blocks * width)
    )
    gate_next = jnp.dot(part_rows, gate_local, preferred_element_type=jnp.float32)
    up_next = jnp.dot(part_rows, up_local, preferred_element_type=jnp.float32)
    inner = (jax.nn.silu(gate_next) * up_next).astype(jnp.bfloat16)
    partial_out = jnp.dot(inner, down_local, preferred_element_type=jnp.float32)
    partial_out = (
        partial_out.reshape(expert_count, capacity, feature_blocks, width)
        .transpose(0, 2, 1, 3)
        .reshape(expert_count * feature_blocks, capacity, width)
    )
    pieces = lax.all_to_all(partial_out.astype(jnp.bfloat16), ("expert", "ffn"), 0, 0, tiled=True)
    returned = (
        jnp.sum(pieces.reshape(expert_count, feature_blocks, capacity, width).astype(jnp.float32), axis=1)
        .astype(jnp.bfloat16)
    )
    mixed = jnp.dot(
        combine,
        returned.reshape(expert_count * capacity, -1).astype(jnp.float32),
        precision=lax.Precision.HIGHEST,
    )
    return (hidden + mixed).astype(jnp.bfloat16)


def solution(mesh):
    placed = (
        P(("expert", "ffn"), None),
        P(("expert", "ffn"), None),
        P(("expert", "ffn"), None),
        P(("expert", "ffn"), None, None),
        P(("expert", "ffn"), None, None),
        P(("expert", "ffn")),
        P("expert", "ffn"),
        P(None, "ffn"),
        P("ffn"),
        P("ffn", None),
        P("expert", None, "ffn"),
        P("expert", None, "ffn"),
        P("expert", "ffn", None),
        P("expert", None),
    )
    return jax.shard_map(
        local, mesh=mesh, in_specs=placed, out_specs=P("expert", "ffn"), check_vma=False
    )
```

```python
import math

import jax
import jax.numpy as jnp
from jax import lax
from jax.experimental import pallas as pl
from jax.experimental.pallas import tpu as pltpu
from jax.sharding import PartitionSpec as P

D = 4096
QH = 32
KVH = 8
HD = 128
CACHE = 512


EPSILON = 1e-05
FLOOR = -1e30


def butterfly_sum(value, axis_name):
    size = lax.axis_size(axis_name)
    step = 1
    while step < size:
        pairs = [(j, j ^ step) for j in range(size)]
        value = value + lax.ppermute(value, axis_name, pairs)
        step *= 2
    return value


def gather_by_exchange(value, axis_name):
    size = lax.axis_size(axis_name)
    copies = jnp.broadcast_to(value[None], (size,) + value.shape)
    return lax.all_to_all(copies, axis_name, 0, 0, tiled=True)


def gate_up_kernel(rows_ref, gate_ref, up_ref, out_ref, gate_acc, up_acc):
    step = pl.program_id(0)
    groups, blocks, capacity, width = rows_ref.shape

    @pl.when(step == 0)
    def _():
        gate_acc[...] = jnp.zeros_like(gate_acc)
        up_acc[...] = jnp.zeros_like(up_acc)

    for block in range(blocks):
        rows = rows_ref[:, block].reshape(groups * capacity, width)
        gate_acc[...] += jnp.dot(
            rows, gate_ref[block * width:(block + 1) * width, :], preferred_element_type=jnp.float32
        )
        up_acc[...] += jnp.dot(
            rows, up_ref[block * width:(block + 1) * width, :], preferred_element_type=jnp.float32
        )

    @pl.when(step == pl.num_programs(0) - 1)
    def _():
        gate_sum = gate_acc[...]
        out_ref[...] = (gate_sum / (1.0 + jnp.exp(-gate_sum)) * up_acc[...]).astype(out_ref.dtype)


def gate_up(rows, gate_local, up_local):
    groups, blocks, capacity, width = rows.shape
    per_step = 4
    hidden_units = gate_local.shape[1]
    row_count = groups * capacity
    return pl.pallas_call(
        gate_up_kernel,
        out_shape=jax.ShapeDtypeStruct((row_count, hidden_units), jnp.bfloat16),
        grid=(blocks // per_step,),
        in_specs=[
            pl.BlockSpec((groups, per_step, capacity, width), lambda j: (0, j, 0, 0)),
            pl.BlockSpec((per_step * width, hidden_units), lambda j: (j, 0)),
            pl.BlockSpec((per_step * width, hidden_units), lambda j: (j, 0)),
        ],
        out_specs=pl.BlockSpec((row_count, hidden_units), lambda j: (0, 0)),
        scratch_shapes=[
            pltpu.VMEM((row_count, hidden_units), jnp.float32),
            pltpu.VMEM((row_count, hidden_units), jnp.float32),
        ],
        compiler_params=pltpu.CompilerParams(dimension_semantics=("arbitrary",)),
        cost_estimate=pl.CostEstimate(
            flops=4 * row_count * blocks * width * hidden_units,
            transcendentals=row_count * hidden_units,
            bytes_accessed=2 * (rows.size + gate_local.size + up_local.size + row_count * hidden_units),
        ),
    )(rows, gate_local, up_local)


def attend_local(queries, new_keys, new_values, key_cache, value_cache, lengths):
    request_count = queries.shape[0]
    group_size = QH // KVH
    score_scale = 1.0 / math.sqrt(HD)
    query_heads = queries.reshape(request_count, KVH, group_size, HD)
    head_eye = jnp.eye(KVH, dtype=queries.dtype)[None, :, None, :, None]
    spread_queries = (query_heads[:, :, :, None, :] * head_eye).reshape(request_count, QH, KVH * HD)
    scores = (
        jnp.einsum("rhc,rpc->rhp", spread_queries, key_cache, preferred_element_type=jnp.float32)
        * score_scale
    )
    score_new = (
        jnp.einsum("rhc,rc->rh", spread_queries, new_keys, preferred_element_type=jnp.float32)
        * score_scale
    )
    positions = jnp.arange(key_cache.shape[1], dtype=jnp.int32)
    live_mask = (positions[None, :] < lengths[:, None])[:, None, :]
    masked = jnp.where(live_mask, scores, FLOOR)
    largest = jnp.maximum(jnp.max(masked, axis=-1), score_new)
    weights = jnp.where(live_mask, jnp.exp(masked - largest[..., None]), 0.0)
    weight_new = jnp.exp(score_new - largest)
    denoms = jnp.sum(weights, axis=-1) + weight_new
    rounded_new = weight_new.astype(jnp.bfloat16).astype(jnp.float32)
    spread_totals = jnp.einsum(
        "rhp,rpc->rhc", weights.astype(jnp.bfloat16), value_cache, preferred_element_type=jnp.float32
    ) + rounded_new[..., None] * new_values[:, None, :].astype(jnp.float32)
    spread_totals = spread_totals / denoms[..., None]
    totals = jnp.sum(
        spread_totals.reshape(request_count, KVH, group_size, KVH, HD) * head_eye.astype(jnp.float32),
        axis=3,
    )
    return totals.astype(jnp.bfloat16).reshape(request_count, QH * HD)


def local(
    queries,
    new_keys,
    new_values,
    key_cache,
    value_cache,
    lengths,
    residual,
    out_weight,
    norm_gain,
    router,
    gate_weight,
    up_weight,
    down_weight,
    routes,
):
    attended = attend_local(queries, new_keys, new_values, key_cache, value_cache, lengths)
    gathered = gather_by_exchange(attended, "ffn").reshape(-1, attended.shape[1])
    hidden = residual.astype(jnp.float32) + jnp.dot(
        gathered,
        out_weight,
        preferred_element_type=jnp.float32,
    )
    scaled = hidden * norm_gain
    square_part = jnp.sum(hidden * hidden, axis=-1, keepdims=True)
    logit_part = jnp.dot(scaled, router, precision=lax.Precision.HIGHEST)
    stats = jnp.sum(
        gather_by_exchange(jnp.concatenate([square_part, logit_part], axis=1), "ffn"), axis=0
    )
    inverse = lax.rsqrt(stats[:, :1] / D + EPSILON)
    logits = stats[:, 1:] * inverse
    normed = (scaled * inverse).astype(jnp.bfloat16)
    expert_count = lax.axis_size("expert")
    row_count = routes.shape[0]
    capacity = row_count // 2
    expert_ids = jnp.arange(expert_count, dtype=jnp.int32)
    chosen = routes[:, :, None] == expert_ids[None, None, :]
    picked = jnp.sum(jnp.where(chosen, logits[:, None, :], 0.0), axis=-1)
    first_weight = jax.nn.sigmoid(picked[:, 0] - picked[:, 1])
    route_weights = jnp.stack([first_weight, 1.0 - first_weight], axis=1)
    flat_hits = chosen.astype(jnp.int32).reshape(row_count * 2, expert_count)
    earlier = jnp.cumsum(flat_hits, axis=0) - flat_hits
    slots = jnp.sum(earlier * flat_hits, axis=-1).reshape(row_count, 2)
    targets = routes * capacity + slots
    slot_ids = jnp.arange(expert_count * capacity, dtype=jnp.int32)
    slot_hits = slot_ids[:, None, None] == targets[None, :, :]
    dispatch = jnp.sum(slot_hits.astype(jnp.float32), axis=-1).astype(jnp.bfloat16)
    combine = jnp.sum(jnp.where(slot_hits, route_weights[None, :, :], 0.0), axis=-1).T
    gate_local = gate_weight[0]
    up_local = up_weight[0]
    down_local = down_weight[0]
    share_rows = (
        jnp.dot(dispatch, normed, preferred_element_type=jnp.float32)
        .astype(jnp.bfloat16)
        .reshape(expert_count, capacity, normed.shape[1])
    )
    feature_blocks = lax.axis_size("ffn")
    width = normed.shape[1]
    outgoing = jnp.broadcast_to(
        share_rows[:, None], (expert_count, feature_blocks, capacity, width)
    ).reshape(expert_count * feature_blocks, capacity, width)
    incoming = lax.all_to_all(outgoing, ("expert", "ffn"), 0, 0, tiled=True)
    inner = gate_up(
        incoming.reshape(expert_count, feature_blocks, capacity, width), gate_local, up_local
    )
    partial_out = jnp.dot(inner, down_local, preferred_element_type=jnp.float32)
    partial_out = (
        partial_out.reshape(expert_count, capacity, feature_blocks, width)
        .transpose(0, 2, 1, 3)
        .reshape(expert_count * feature_blocks, capacity, width)
    )
    pieces = lax.all_to_all(partial_out.astype(jnp.bfloat16), ("expert", "ffn"), 0, 0, tiled=True)
    returned = (
        jnp.sum(pieces.reshape(expert_count, feature_blocks, capacity, width).astype(jnp.float32), axis=1)
        .astype(jnp.bfloat16)
    )
    mixed = jnp.dot(
        combine,
        returned.reshape(expert_count * capacity, -1).astype(jnp.float32),
        precision=lax.Precision.HIGHEST,
    )
    return (hidden + mixed).astype(jnp.bfloat16)


def solution(mesh):
    placed = (
        P(("expert", "ffn"), None),
        P(("expert", "ffn"), None),
        P(("expert", "ffn"), None),
        P(("expert", "ffn"), None, None),
        P(("expert", "ffn"), None, None),
        P(("expert", "ffn")),
        P("expert", "ffn"),
        P(None, "ffn"),
        P("ffn"),
        P("ffn", None),
        P("expert", None, "ffn"),
        P("expert", None, "ffn"),
        P("expert", "ffn", None),
        P("expert", None),
    )
    return jax.shard_map(
        local, mesh=mesh, in_specs=placed, out_specs=P("expert", "ffn"), check_vma=False
    )
```

```python
import math

import jax
import jax.numpy as jnp
from jax import lax
from jax.experimental import pallas as pl
from jax.experimental.pallas import tpu as pltpu
from jax.sharding import PartitionSpec as P

D = 4096
QH = 32
KVH = 8
HD = 128
CACHE = 512


EPSILON = 1e-05
FLOOR = -1e30


def butterfly_sum(value, axis_name):
    size = lax.axis_size(axis_name)
    step = 1
    while step < size:
        pairs = [(j, j ^ step) for j in range(size)]
        value = value + lax.ppermute(value, axis_name, pairs)
        step *= 2
    return value


def gather_by_exchange(value, axis_name):
    size = lax.axis_size(axis_name)
    copies = jnp.broadcast_to(value[None], (size,) + value.shape)
    return lax.all_to_all(copies, axis_name, 0, 0, tiled=True)


def expert_kernel(rows_hbm, gate_hbm, up_hbm, down_hbm, out_ref, rows_v, gate_v, up_v, down_v, sems):
    groups, blocks, capacity, width = rows_v.shape
    row_count = groups * capacity
    hidden_units = gate_v.shape[1]
    copies = []
    for block in range(blocks):
        span = pl.ds(block * width, width)
        trio = (
            pltpu.make_async_copy(rows_hbm.at[:, block], rows_v.at[:, block], sems.at[0, block]),
            pltpu.make_async_copy(gate_hbm.at[span], gate_v.at[span], sems.at[1, block]),
            pltpu.make_async_copy(up_hbm.at[span], up_v.at[span], sems.at[2, block]),
        )
        for copy in trio:
            copy.start()
        copies.append(trio)
    down_copy = pltpu.make_async_copy(down_hbm, down_v, sems.at[3, 0])
    down_copy.start()
    gate_sum = jnp.zeros((row_count, hidden_units), jnp.float32)
    up_sum = jnp.zeros((row_count, hidden_units), jnp.float32)
    for block in range(blocks):
        for copy in copies[block]:
            copy.wait()
        rows = rows_v[:, block].reshape(row_count, width)
        span = pl.ds(block * width, width)
        gate_sum += jnp.dot(rows, gate_v[span, :], preferred_element_type=jnp.float32)
        up_sum += jnp.dot(rows, up_v[span, :], preferred_element_type=jnp.float32)
    inner = (gate_sum / (1.0 + jnp.exp(-gate_sum)) * up_sum).astype(jnp.bfloat16)
    down_copy.wait()
    for block in range(blocks):
        part = jnp.dot(inner, down_v[:, pl.ds(block * width, width)], preferred_element_type=jnp.float32)
        out_ref[:, block] = part.astype(out_ref.dtype).reshape(groups, capacity, width)


def expert_block(rows, gate_local, up_local, down_local):
    groups, blocks, capacity, width = rows.shape
    hidden_units = gate_local.shape[1]
    row_count = groups * capacity
    anywhere = pl.BlockSpec(memory_space=pl.ANY)
    return pl.pallas_call(
        expert_kernel,
        out_shape=jax.ShapeDtypeStruct(rows.shape, jnp.bfloat16),
        in_specs=[anywhere, anywhere, anywhere, anywhere],
        out_specs=pl.BlockSpec(memory_space=pltpu.VMEM),
        scratch_shapes=[
            pltpu.VMEM(rows.shape, rows.dtype),
            pltpu.VMEM(gate_local.shape, gate_local.dtype),
            pltpu.VMEM(up_local.shape, up_local.dtype),
            pltpu.VMEM(down_local.shape, down_local.dtype),
            pltpu.SemaphoreType.DMA((4, blocks)),
        ],
        compiler_params=pltpu.CompilerParams(vmem_limit_bytes=48 * 1024 * 1024),
        cost_estimate=pl.CostEstimate(
            flops=6 * row_count * blocks * width * hidden_units,
            transcendentals=row_count * hidden_units,
            bytes_accessed=2 * (2 * rows.size + gate_local.size + up_local.size + down_local.size),
        ),
    )(rows, gate_local, up_local, down_local)


def attend_local(queries, new_keys, new_values, key_cache, value_cache, lengths):
    request_count = queries.shape[0]
    group_size = QH // KVH
    score_scale = 1.0 / math.sqrt(HD)
    query_heads = queries.reshape(request_count, KVH, group_size, HD)
    head_eye = jnp.eye(KVH, dtype=queries.dtype)[None, :, None, :, None]
    spread_queries = (query_heads[:, :, :, None, :] * head_eye).reshape(request_count, QH, KVH * HD)
    scores = (
        jnp.einsum("rhc,rpc->rhp", spread_queries, key_cache, preferred_element_type=jnp.float32)
        * score_scale
    )
    score_new = (
        jnp.einsum("rhc,rc->rh", spread_queries, new_keys, preferred_element_type=jnp.float32)
        * score_scale
    )
    positions = jnp.arange(key_cache.shape[1], dtype=jnp.int32)
    live_mask = (positions[None, :] < lengths[:, None])[:, None, :]
    masked = jnp.where(live_mask, scores, FLOOR)
    largest = jnp.maximum(jnp.max(masked, axis=-1), score_new)
    weights = jnp.where(live_mask, jnp.exp(masked - largest[..., None]), 0.0)
    weight_new = jnp.exp(score_new - largest)
    denoms = jnp.sum(weights, axis=-1) + weight_new
    rounded_new = weight_new.astype(jnp.bfloat16).astype(jnp.float32)
    spread_totals = jnp.einsum(
        "rhp,rpc->rhc", weights.astype(jnp.bfloat16), value_cache, preferred_element_type=jnp.float32
    ) + rounded_new[..., None] * new_values[:, None, :].astype(jnp.float32)
    spread_totals = spread_totals / denoms[..., None]
    totals = jnp.sum(
        spread_totals.reshape(request_count, KVH, group_size, KVH, HD) * head_eye.astype(jnp.float32),
        axis=3,
    )
    return totals.astype(jnp.bfloat16).reshape(request_count, QH * HD)


def local(
    queries,
    new_keys,
    new_values,
    key_cache,
    value_cache,
    lengths,
    residual,
    out_weight,
    norm_gain,
    router,
    gate_weight,
    up_weight,
    down_weight,
    routes,
):
    attended = attend_local(queries, new_keys, new_values, key_cache, value_cache, lengths)
    gathered = gather_by_exchange(attended, "ffn").reshape(-1, attended.shape[1])
    hidden = residual.astype(jnp.float32) + jnp.dot(
        gathered,
        out_weight,
        preferred_element_type=jnp.float32,
    )
    scaled = hidden * norm_gain
    square_part = jnp.sum(hidden * hidden, axis=-1, keepdims=True)
    logit_part = jnp.dot(scaled, router, precision=lax.Precision.HIGHEST)
    stats = jnp.sum(
        gather_by_exchange(jnp.concatenate([square_part, logit_part], axis=1), "ffn"), axis=0
    )
    inverse = lax.rsqrt(stats[:, :1] / D + EPSILON)
    logits = stats[:, 1:] * inverse
    normed = (scaled * inverse).astype(jnp.bfloat16)
    expert_count = lax.axis_size("expert")
    row_count = routes.shape[0]
    capacity = row_count // 2
    expert_ids = jnp.arange(expert_count, dtype=jnp.int32)
    chosen = routes[:, :, None] == expert_ids[None, None, :]
    picked = jnp.sum(jnp.where(chosen, logits[:, None, :], 0.0), axis=-1)
    first_weight = jax.nn.sigmoid(picked[:, 0] - picked[:, 1])
    route_weights = jnp.stack([first_weight, 1.0 - first_weight], axis=1)
    flat_hits = chosen.astype(jnp.int32).reshape(row_count * 2, expert_count)
    earlier = jnp.cumsum(flat_hits, axis=0) - flat_hits
    slots = jnp.sum(earlier * flat_hits, axis=-1).reshape(row_count, 2)
    targets = routes * capacity + slots
    slot_ids = jnp.arange(expert_count * capacity, dtype=jnp.int32)
    slot_hits = slot_ids[:, None, None] == targets[None, :, :]
    dispatch = jnp.sum(slot_hits.astype(jnp.float32), axis=-1).astype(jnp.bfloat16)
    combine = jnp.sum(jnp.where(slot_hits, route_weights[None, :, :], 0.0), axis=-1).T
    gate_local = gate_weight[0]
    up_local = up_weight[0]
    down_local = down_weight[0]
    share_rows = (
        jnp.dot(dispatch, normed, preferred_element_type=jnp.float32)
        .astype(jnp.bfloat16)
        .reshape(expert_count, capacity, normed.shape[1])
    )
    feature_blocks = lax.axis_size("ffn")
    width = normed.shape[1]
    outgoing = jnp.broadcast_to(
        share_rows[:, None], (expert_count, feature_blocks, capacity, width)
    ).reshape(expert_count * feature_blocks, capacity, width)
    incoming = lax.all_to_all(outgoing, ("expert", "ffn"), 0, 0, tiled=True)
    partial_out = expert_block(
        incoming.reshape(expert_count, feature_blocks, capacity, width), gate_local, up_local, down_local
    ).reshape(expert_count * feature_blocks, capacity, width)
    pieces = lax.all_to_all(partial_out, ("expert", "ffn"), 0, 0, tiled=True)
    returned = (
        jnp.sum(pieces.reshape(expert_count, feature_blocks, capacity, width).astype(jnp.float32), axis=1)
        .astype(jnp.bfloat16)
    )
    mixed = jnp.dot(
        combine,
        returned.reshape(expert_count * capacity, -1).astype(jnp.float32),
        precision=lax.Precision.HIGHEST,
    )
    return (hidden + mixed).astype(jnp.bfloat16)


def solution(mesh):
    placed = (
        P(("expert", "ffn"), None),
        P(("expert", "ffn"), None),
        P(("expert", "ffn"), None),
        P(("expert", "ffn"), None, None),
        P(("expert", "ffn"), None, None),
        P(("expert", "ffn")),
        P("expert", "ffn"),
        P(None, "ffn"),
        P("ffn"),
        P("ffn", None),
        P("expert", None, "ffn"),
        P("expert", None, "ffn"),
        P("expert", "ffn", None),
        P("expert", None),
    )
    return jax.shard_map(
        local, mesh=mesh, in_specs=placed, out_specs=P("expert", "ffn"), check_vma=False
    )
```

```python
import math

import jax
import jax.numpy as jnp
from jax import lax
from jax.experimental import pallas as pl
from jax.experimental.pallas import tpu as pltpu
from jax.sharding import PartitionSpec as P

D = 4096
QH = 32
KVH = 8
HD = 128
CACHE = 512


EPSILON = 1e-05
FLOOR = -1e30


def butterfly_sum(value, axis_name):
    size = lax.axis_size(axis_name)
    step = 1
    while step < size:
        pairs = [(j, j ^ step) for j in range(size)]
        value = value + lax.ppermute(value, axis_name, pairs)
        step *= 2
    return value


def gather_by_exchange(value, axis_name):
    size = lax.axis_size(axis_name)
    copies = jnp.broadcast_to(value[None], (size,) + value.shape)
    return lax.all_to_all(copies, axis_name, 0, 0, tiled=True)


def expert_kernel(rows_hbm, gate_hbm, up_hbm, down_hbm, out_ref, rows_v, gate_v, up_v, down_v, sems):
    groups, blocks, capacity, width = rows_v.shape
    row_count = groups * capacity
    hidden_units = gate_v.shape[1]
    copies = []
    for block in range(blocks):
        span = pl.ds(block * width, width)
        trio = (
            pltpu.make_async_copy(rows_hbm.at[:, block], rows_v.at[:, block], sems.at[0, block]),
            pltpu.make_async_copy(gate_hbm.at[span], gate_v.at[span], sems.at[1, block]),
            pltpu.make_async_copy(up_hbm.at[span], up_v.at[span], sems.at[2, block]),
        )
        for copy in trio:
            copy.start()
        copies.append(trio)
    down_copy = pltpu.make_async_copy(down_hbm, down_v, sems.at[3, 0])
    down_copy.start()
    gate_sum = jnp.zeros((row_count, hidden_units), jnp.float32)
    up_sum = jnp.zeros((row_count, hidden_units), jnp.float32)
    for block in range(blocks):
        for copy in copies[block]:
            copy.wait()
        rows = rows_v[:, block].reshape(row_count, width)
        span = pl.ds(block * width, width)
        gate_sum += jnp.dot(rows, gate_v[span, :], preferred_element_type=jnp.float32)
        up_sum += jnp.dot(rows, up_v[span, :], preferred_element_type=jnp.float32)
    inner = (gate_sum / (1.0 + jnp.exp(-gate_sum)) * up_sum).astype(jnp.bfloat16)
    down_copy.wait()
    for block in range(blocks):
        part = jnp.dot(inner, down_v[:, pl.ds(block * width, width)], preferred_element_type=jnp.float32)
        out_ref[:, block] = part.astype(out_ref.dtype).reshape(groups, capacity, width)


def expert_block(rows, gate_local, up_local, down_local):
    groups, blocks, capacity, width = rows.shape
    hidden_units = gate_local.shape[1]
    row_count = groups * capacity
    anywhere = pl.BlockSpec(memory_space=pl.ANY)
    return pl.pallas_call(
        expert_kernel,
        out_shape=jax.ShapeDtypeStruct(rows.shape, jnp.bfloat16),
        in_specs=[anywhere, anywhere, anywhere, anywhere],
        out_specs=pl.BlockSpec(memory_space=pltpu.VMEM),
        scratch_shapes=[
            pltpu.VMEM(rows.shape, rows.dtype),
            pltpu.VMEM(gate_local.shape, gate_local.dtype),
            pltpu.VMEM(up_local.shape, up_local.dtype),
            pltpu.VMEM(down_local.shape, down_local.dtype),
            pltpu.SemaphoreType.DMA((4, blocks)),
        ],
        compiler_params=pltpu.CompilerParams(vmem_limit_bytes=48 * 1024 * 1024),
        cost_estimate=pl.CostEstimate(
            flops=6 * row_count * blocks * width * hidden_units,
            transcendentals=row_count * hidden_units,
            bytes_accessed=2 * (2 * rows.size + gate_local.size + up_local.size + down_local.size),
        ),
    )(rows, gate_local, up_local, down_local)


def attend_kernel(
    lengths_ref, queries_ref, new_keys_ref, new_values_ref, keys_hbm, values_hbm, out_ref, keys_v, values_v, sems
):
    request_count, heads, width = queries_ref.shape
    group_size = heads // KVH
    score_scale = 1.0 / math.sqrt(HD)
    copies = []
    for request in range(request_count):
        pair = (
            pltpu.make_async_copy(keys_hbm.at[request], keys_v.at[request], sems.at[0, request]),
            pltpu.make_async_copy(values_hbm.at[request], values_v.at[request], sems.at[1, request]),
        )
        for copy in pair:
            copy.start()
        copies.append(pair)
    head_group = lax.broadcasted_iota(jnp.int32, (heads, 1), 0) // group_size
    for request in range(request_count):
        for copy in copies[request]:
            copy.wait()
        spread = queries_ref[request]
        scores = lax.dot_general(
            spread, keys_v[request], (((1,), (1,)), ((), ())), preferred_element_type=jnp.float32
        ) * score_scale
        key_new = new_keys_ref[pl.ds(request, 1), :].astype(jnp.float32)
        score_new = jnp.sum(spread.astype(jnp.float32) * key_new, axis=1, keepdims=True) * score_scale
        positions = lax.broadcasted_iota(jnp.int32, scores.shape, 1)
        live = positions < lengths_ref[request]
        masked = jnp.where(live, scores, FLOOR)
        largest = jnp.maximum(jnp.max(masked, axis=1, keepdims=True), score_new)
        weights = jnp.where(live, jnp.exp(masked - largest), 0.0)
        weight_new = jnp.exp(score_new - largest)
        denoms = jnp.sum(weights, axis=1, keepdims=True) + weight_new
        rounded_new = weight_new.astype(jnp.bfloat16).astype(jnp.float32)
        totals = jnp.dot(weights.astype(jnp.bfloat16), values_v[request], preferred_element_type=jnp.float32)
        totals = totals + rounded_new * new_values_ref[pl.ds(request, 1), :].astype(jnp.float32)
        totals = totals / denoms
        picked = jnp.zeros((heads, HD), jnp.float32)
        for head in range(KVH):
            picked = picked + jnp.where(head_group == head, totals[:, head * HD:(head + 1) * HD], 0.0)
        out_ref[request] = picked.astype(out_ref.dtype)


def attend_local(queries, new_keys, new_values, key_cache, value_cache, lengths):
    request_count = queries.shape[0]
    group_size = QH // KVH
    query_heads = queries.reshape(request_count, KVH, group_size, HD)
    head_eye = jnp.eye(KVH, dtype=queries.dtype)[None, :, None, :, None]
    spread_queries = (query_heads[:, :, :, None, :] * head_eye).reshape(request_count, QH, KVH * HD)
    anywhere = pl.BlockSpec(memory_space=pl.ANY)
    whole = pl.BlockSpec(memory_space=pltpu.VMEM)
    attended = pl.pallas_call(
        attend_kernel,
        out_shape=jax.ShapeDtypeStruct((request_count, QH, HD), jnp.bfloat16),
        in_specs=[pl.BlockSpec(memory_space=pltpu.SMEM), whole, whole, whole, anywhere, anywhere],
        out_specs=whole,
        scratch_shapes=[
            pltpu.VMEM(key_cache.shape, key_cache.dtype),
            pltpu.VMEM(value_cache.shape, value_cache.dtype),
            pltpu.SemaphoreType.DMA((2, request_count)),
        ],
        compiler_params=pltpu.CompilerParams(vmem_limit_bytes=40 * 1024 * 1024),
        cost_estimate=pl.CostEstimate(
            flops=4 * request_count * QH * key_cache.shape[1] * key_cache.shape[2],
            transcendentals=request_count * QH * key_cache.shape[1],
            bytes_accessed=2 * (key_cache.size + value_cache.size),
        ),
    )(lengths, spread_queries, new_keys, new_values, key_cache, value_cache)
    return attended.reshape(request_count, QH * HD)


def local(
    queries,
    new_keys,
    new_values,
    key_cache,
    value_cache,
    lengths,
    residual,
    out_weight,
    norm_gain,
    router,
    gate_weight,
    up_weight,
    down_weight,
    routes,
):
    attended = attend_local(queries, new_keys, new_values, key_cache, value_cache, lengths)
    gathered = gather_by_exchange(attended, "ffn").reshape(-1, attended.shape[1])
    hidden = residual.astype(jnp.float32) + jnp.dot(
        gathered,
        out_weight,
        preferred_element_type=jnp.float32,
    )
    scaled = hidden * norm_gain
    square_part = jnp.sum(hidden * hidden, axis=-1, keepdims=True)
    logit_part = jnp.dot(scaled, router, precision=lax.Precision.HIGHEST)
    stats = jnp.sum(
        gather_by_exchange(jnp.concatenate([square_part, logit_part], axis=1), "ffn"), axis=0
    )
    inverse = lax.rsqrt(stats[:, :1] / D + EPSILON)
    logits = stats[:, 1:] * inverse
    normed = (scaled * inverse).astype(jnp.bfloat16)
    expert_count = lax.axis_size("expert")
    row_count = routes.shape[0]
    capacity = row_count // 2
    expert_ids = jnp.arange(expert_count, dtype=jnp.int32)
    chosen = routes[:, :, None] == expert_ids[None, None, :]
    picked = jnp.sum(jnp.where(chosen, logits[:, None, :], 0.0), axis=-1)
    first_weight = jax.nn.sigmoid(picked[:, 0] - picked[:, 1])
    route_weights = jnp.stack([first_weight, 1.0 - first_weight], axis=1)
    flat_hits = chosen.astype(jnp.int32).reshape(row_count * 2, expert_count)
    earlier = jnp.cumsum(flat_hits, axis=0) - flat_hits
    slots = jnp.sum(earlier * flat_hits, axis=-1).reshape(row_count, 2)
    targets = routes * capacity + slots
    slot_ids = jnp.arange(expert_count * capacity, dtype=jnp.int32)
    slot_hits = slot_ids[:, None, None] == targets[None, :, :]
    dispatch = jnp.sum(slot_hits.astype(jnp.float32), axis=-1).astype(jnp.bfloat16)
    combine = jnp.sum(jnp.where(slot_hits, route_weights[None, :, :], 0.0), axis=-1).T
    gate_local = gate_weight[0]
    up_local = up_weight[0]
    down_local = down_weight[0]
    share_rows = (
        jnp.dot(dispatch, normed, preferred_element_type=jnp.float32)
        .astype(jnp.bfloat16)
        .reshape(expert_count, capacity, normed.shape[1])
    )
    feature_blocks = lax.axis_size("ffn")
    width = normed.shape[1]
    outgoing = jnp.broadcast_to(
        share_rows[:, None], (expert_count, feature_blocks, capacity, width)
    ).reshape(expert_count * feature_blocks, capacity, width)
    incoming = lax.all_to_all(outgoing, ("expert", "ffn"), 0, 0, tiled=True)
    partial_out = expert_block(
        incoming.reshape(expert_count, feature_blocks, capacity, width), gate_local, up_local, down_local
    ).reshape(expert_count * feature_blocks, capacity, width)
    pieces = lax.all_to_all(partial_out, ("expert", "ffn"), 0, 0, tiled=True)
    returned = (
        jnp.sum(pieces.reshape(expert_count, feature_blocks, capacity, width).astype(jnp.float32), axis=1)
        .astype(jnp.bfloat16)
    )
    mixed = jnp.dot(
        combine,
        returned.reshape(expert_count * capacity, -1).astype(jnp.float32),
        precision=lax.Precision.HIGHEST,
    )
    return (hidden + mixed).astype(jnp.bfloat16)


def solution(mesh):
    placed = (
        P(("expert", "ffn"), None),
        P(("expert", "ffn"), None),
        P(("expert", "ffn"), None),
        P(("expert", "ffn"), None, None),
        P(("expert", "ffn"), None, None),
        P(("expert", "ffn")),
        P("expert", "ffn"),
        P(None, "ffn"),
        P("ffn"),
        P("ffn", None),
        P("expert", None, "ffn"),
        P("expert", None, "ffn"),
        P("expert", "ffn", None),
        P("expert", None),
    )
    return jax.shard_map(
        local, mesh=mesh, in_specs=placed, out_specs=P("expert", "ffn"), check_vma=False
    )
```

```python
import math

import jax
import jax.numpy as jnp
from jax import lax
from jax.experimental import pallas as pl
from jax.experimental.pallas import tpu as pltpu
from jax.sharding import PartitionSpec as P

D = 4096
QH = 32
KVH = 8
HD = 128
CACHE = 512


EPSILON = 1e-05
FLOOR = -1e30


def butterfly_sum(value, axis_name):
    size = lax.axis_size(axis_name)
    step = 1
    while step < size:
        pairs = [(j, j ^ step) for j in range(size)]
        value = value + lax.ppermute(value, axis_name, pairs)
        step *= 2
    return value


def gather_by_exchange(value, axis_name):
    size = lax.axis_size(axis_name)
    copies = jnp.broadcast_to(value[None], (size,) + value.shape)
    return lax.all_to_all(copies, axis_name, 0, 0, tiled=True)


def expert_kernel(rows_hbm, gate_hbm, up_hbm, down_hbm, out_ref, rows_v, gate_v, up_v, down_v, sems):
    groups, blocks, capacity, width = rows_v.shape
    row_count = groups * capacity
    hidden_units = gate_v.shape[1]
    copies = []
    for block in range(blocks):
        span = pl.ds(block * width, width)
        trio = (
            pltpu.make_async_copy(rows_hbm.at[:, block], rows_v.at[:, block], sems.at[0, block]),
            pltpu.make_async_copy(gate_hbm.at[span], gate_v.at[span], sems.at[1, block]),
            pltpu.make_async_copy(up_hbm.at[span], up_v.at[span], sems.at[2, block]),
        )
        for copy in trio:
            copy.start()
        copies.append(trio)
    down_copy = pltpu.make_async_copy(down_hbm, down_v, sems.at[3, 0])
    down_copy.start()
    gate_sum = jnp.zeros((row_count, hidden_units), jnp.float32)
    up_sum = jnp.zeros((row_count, hidden_units), jnp.float32)
    for block in range(blocks):
        for copy in copies[block]:
            copy.wait()
        rows = rows_v[:, block].reshape(row_count, width)
        span = pl.ds(block * width, width)
        gate_sum += jnp.dot(rows, gate_v[span, :], preferred_element_type=jnp.float32)
        up_sum += jnp.dot(rows, up_v[span, :], preferred_element_type=jnp.float32)
    inner = (gate_sum / (1.0 + jnp.exp(-gate_sum)) * up_sum).astype(jnp.bfloat16)
    down_copy.wait()
    for block in range(blocks):
        part = jnp.dot(inner, down_v[:, pl.ds(block * width, width)], preferred_element_type=jnp.float32)
        out_ref[:, block] = part.astype(out_ref.dtype).reshape(groups, capacity, width)


def expert_block(rows, gate_local, up_local, down_local):
    groups, blocks, capacity, width = rows.shape
    hidden_units = gate_local.shape[1]
    row_count = groups * capacity
    anywhere = pl.BlockSpec(memory_space=pltpu.HBM)
    return pl.pallas_call(
        expert_kernel,
        out_shape=jax.ShapeDtypeStruct(rows.shape, jnp.bfloat16),
        in_specs=[anywhere, anywhere, anywhere, anywhere],
        out_specs=pl.BlockSpec(memory_space=pltpu.VMEM),
        scratch_shapes=[
            pltpu.VMEM(rows.shape, rows.dtype),
            pltpu.VMEM(gate_local.shape, gate_local.dtype),
            pltpu.VMEM(up_local.shape, up_local.dtype),
            pltpu.VMEM(down_local.shape, down_local.dtype),
            pltpu.SemaphoreType.DMA((4, blocks)),
        ],
        compiler_params=pltpu.CompilerParams(vmem_limit_bytes=48 * 1024 * 1024),
        cost_estimate=pl.CostEstimate(
            flops=6 * row_count * blocks * width * hidden_units,
            transcendentals=row_count * hidden_units,
            bytes_accessed=2 * (2 * rows.size + gate_local.size + up_local.size + down_local.size),
        ),
    )(rows, gate_local, up_local, down_local)


def attend_kernel(length_ref, spread_ref, key_new_ref, value_new_ref, keys_ref, values_ref, out_ref):
    heads = spread_ref.shape[0]
    group_size = heads // KVH
    score_scale = 1.0 / math.sqrt(HD)
    head_group = lax.broadcasted_iota(jnp.int32, (heads, 1), 0) // group_size
    spread = spread_ref[...]
    scores = lax.dot_general(
        spread, keys_ref[...], (((1,), (1,)), ((), ())), preferred_element_type=jnp.float32
    ) * score_scale
    key_new = key_new_ref[...].astype(jnp.float32)
    score_new = jnp.sum(spread.astype(jnp.float32) * key_new, axis=1, keepdims=True) * score_scale
    positions = lax.broadcasted_iota(jnp.int32, scores.shape, 1)
    live = positions < length_ref[0]
    masked = jnp.where(live, scores, FLOOR)
    largest = jnp.maximum(jnp.max(masked, axis=1, keepdims=True), score_new)
    weights = jnp.where(live, jnp.exp(masked - largest), 0.0)
    weight_new = jnp.exp(score_new - largest)
    denoms = jnp.sum(weights, axis=1, keepdims=True) + weight_new
    rounded_new = weight_new.astype(jnp.bfloat16).astype(jnp.float32)
    totals = jnp.dot(weights.astype(jnp.bfloat16), values_ref[...], preferred_element_type=jnp.float32)
    totals = totals + rounded_new * value_new_ref[...].astype(jnp.float32)
    totals = totals / denoms
    picked = jnp.zeros((heads, HD), jnp.float32)
    for head in range(KVH):
        picked = picked + jnp.where(head_group == head, totals[:, head * HD:(head + 1) * HD], 0.0)
    out_ref[...] = picked.astype(out_ref.dtype)


def attend_one(length, spread, key_new, value_new, keys, values):
    whole = pl.BlockSpec(memory_space=pltpu.VMEM)
    return pl.pallas_call(
        attend_kernel,
        out_shape=jax.ShapeDtypeStruct((spread.shape[0], HD), jnp.bfloat16),
        in_specs=[pl.BlockSpec(memory_space=pltpu.SMEM), whole, whole, whole, whole, whole],
        out_specs=whole,
        cost_estimate=pl.CostEstimate(
            flops=4 * spread.shape[0] * keys.shape[0] * keys.shape[1],
            transcendentals=spread.shape[0] * keys.shape[0],
            bytes_accessed=2 * (keys.size + values.size),
        ),
    )(length, spread, key_new, value_new, keys, values)


def attend_local(queries, new_keys, new_values, key_cache, value_cache, lengths):
    request_count = queries.shape[0]
    group_size = QH // KVH
    query_heads = queries.reshape(request_count, KVH, group_size, HD)
    head_eye = jnp.eye(KVH, dtype=queries.dtype)[None, :, None, :, None]
    spread_queries = (query_heads[:, :, :, None, :] * head_eye).reshape(request_count, QH, KVH * HD)
    rows = [
        attend_one(
            lengths[request:request + 1],
            spread_queries[request],
            new_keys[request:request + 1],
            new_values[request:request + 1],
            key_cache[request],
            value_cache[request],
        )
        for request in range(request_count)
    ]
    return jnp.stack(rows).reshape(request_count, QH * HD)


def local(
    queries,
    new_keys,
    new_values,
    key_cache,
    value_cache,
    lengths,
    residual,
    out_weight,
    norm_gain,
    router,
    gate_weight,
    up_weight,
    down_weight,
    routes,
):
    attended = attend_local(queries, new_keys, new_values, key_cache, value_cache, lengths)
    gathered = gather_by_exchange(attended, "ffn").reshape(-1, attended.shape[1])
    hidden = residual.astype(jnp.float32) + jnp.dot(
        gathered,
        out_weight,
        preferred_element_type=jnp.float32,
    )
    scaled = hidden * norm_gain
    square_part = jnp.sum(hidden * hidden, axis=-1, keepdims=True)
    logit_part = jnp.dot(scaled, router, precision=lax.Precision.HIGHEST)
    stats = jnp.sum(
        gather_by_exchange(jnp.concatenate([square_part, logit_part], axis=1), "ffn"), axis=0
    )
    inverse = lax.rsqrt(stats[:, :1] / D + EPSILON)
    logits = stats[:, 1:] * inverse
    normed = (scaled * inverse).astype(jnp.bfloat16)
    expert_count = lax.axis_size("expert")
    row_count = routes.shape[0]
    capacity = row_count // 2
    expert_ids = jnp.arange(expert_count, dtype=jnp.int32)
    chosen = routes[:, :, None] == expert_ids[None, None, :]
    picked = jnp.sum(jnp.where(chosen, logits[:, None, :], 0.0), axis=-1)
    first_weight = jax.nn.sigmoid(picked[:, 0] - picked[:, 1])
    route_weights = jnp.stack([first_weight, 1.0 - first_weight], axis=1)
    flat_hits = chosen.astype(jnp.int32).reshape(row_count * 2, expert_count)
    earlier = jnp.cumsum(flat_hits, axis=0) - flat_hits
    slots = jnp.sum(earlier * flat_hits, axis=-1).reshape(row_count, 2)
    targets = routes * capacity + slots
    slot_ids = jnp.arange(expert_count * capacity, dtype=jnp.int32)
    slot_hits = slot_ids[:, None, None] == targets[None, :, :]
    dispatch = jnp.sum(slot_hits.astype(jnp.float32), axis=-1).astype(jnp.bfloat16)
    combine = jnp.sum(jnp.where(slot_hits, route_weights[None, :, :], 0.0), axis=-1).T
    gate_local = gate_weight[0]
    up_local = up_weight[0]
    down_local = down_weight[0]
    share_rows = (
        jnp.dot(dispatch, normed, preferred_element_type=jnp.float32)
        .astype(jnp.bfloat16)
        .reshape(expert_count, capacity, normed.shape[1])
    )
    feature_blocks = lax.axis_size("ffn")
    width = normed.shape[1]
    outgoing = jnp.broadcast_to(
        share_rows[:, None], (expert_count, feature_blocks, capacity, width)
    ).reshape(expert_count * feature_blocks, capacity, width)
    incoming = lax.all_to_all(outgoing, ("expert", "ffn"), 0, 0, tiled=True)
    partial_out = expert_block(
        incoming.reshape(expert_count, feature_blocks, capacity, width), gate_local, up_local, down_local
    ).reshape(expert_count * feature_blocks, capacity, width)
    pieces = lax.all_to_all(partial_out, ("expert", "ffn"), 0, 0, tiled=True)
    returned = (
        jnp.sum(pieces.reshape(expert_count, feature_blocks, capacity, width).astype(jnp.float32), axis=1)
        .astype(jnp.bfloat16)
    )
    mixed = jnp.dot(
        combine,
        returned.reshape(expert_count * capacity, -1).astype(jnp.float32),
        precision=lax.Precision.HIGHEST,
    )
    return (hidden + mixed).astype(jnp.bfloat16)


def solution(mesh):
    placed = (
        P(("expert", "ffn"), None),
        P(("expert", "ffn"), None),
        P(("expert", "ffn"), None),
        P(("expert", "ffn"), None, None),
        P(("expert", "ffn"), None, None),
        P(("expert", "ffn")),
        P("expert", "ffn"),
        P(None, "ffn"),
        P("ffn"),
        P("ffn", None),
        P("expert", None, "ffn"),
        P("expert", None, "ffn"),
        P("expert", "ffn", None),
        P("expert", None),
    )
    return jax.shard_map(
        local, mesh=mesh, in_specs=placed, out_specs=P("expert", "ffn"), check_vma=False
    )
```

```python
import math

import jax
import jax.numpy as jnp
from jax import lax
from jax.experimental import pallas as pl
from jax.experimental.pallas import tpu as pltpu
from jax.sharding import PartitionSpec as P

D = 4096
QH = 32
KVH = 8
HD = 128
CACHE = 512


EPSILON = 1e-05
FLOOR = -1e30


def butterfly_sum(value, axis_name):
    size = lax.axis_size(axis_name)
    step = 1
    while step < size:
        pairs = [(j, j ^ step) for j in range(size)]
        value = value + lax.ppermute(value, axis_name, pairs)
        step *= 2
    return value


def gather_by_exchange(value, axis_name):
    size = lax.axis_size(axis_name)
    copies = jnp.broadcast_to(value[None], (size,) + value.shape)
    return lax.all_to_all(copies, axis_name, 0, 0, tiled=True)


def expert_kernel(rows_hbm, gate_hbm, up_hbm, down_hbm, out_ref, rows_v, gate_v, up_v, down_v, sems):
    groups, blocks, capacity, width = rows_v.shape
    row_count = groups * capacity
    hidden_units = gate_v.shape[1]
    copies = []
    for block in range(blocks):
        span = pl.ds(block * width, width)
        trio = (
            pltpu.make_async_copy(rows_hbm.at[:, block], rows_v.at[:, block], sems.at[0, block]),
            pltpu.make_async_copy(gate_hbm.at[span], gate_v.at[span], sems.at[1, block]),
            pltpu.make_async_copy(up_hbm.at[span], up_v.at[span], sems.at[2, block]),
        )
        for copy in trio:
            copy.start()
        copies.append(trio)
    down_copies = []
    for block in range(blocks):
        span = pl.ds(block * width, width)
        copy = pltpu.make_async_copy(down_hbm.at[:, span], down_v.at[:, span], sems.at[3, block])
        copy.start()
        down_copies.append(copy)
    gate_sum = jnp.zeros((row_count, hidden_units), jnp.float32)
    up_sum = jnp.zeros((row_count, hidden_units), jnp.float32)
    for block in range(blocks):
        for copy in copies[block]:
            copy.wait()
        rows = rows_v[:, block].reshape(row_count, width)
        span = pl.ds(block * width, width)
        gate_sum += jnp.dot(rows, gate_v[span, :], preferred_element_type=jnp.float32)
        up_sum += jnp.dot(rows, up_v[span, :], preferred_element_type=jnp.float32)
    inner = (gate_sum / (1.0 + jnp.exp(-gate_sum)) * up_sum).astype(jnp.bfloat16)
    for block in range(blocks):
        down_copies[block].wait()
        part = jnp.dot(inner, down_v[:, pl.ds(block * width, width)], preferred_element_type=jnp.float32)
        out_ref[:, block] = part.astype(out_ref.dtype).reshape(groups, capacity, width)


def expert_block(rows, gate_local, up_local, down_local):
    groups, blocks, capacity, width = rows.shape
    hidden_units = gate_local.shape[1]
    row_count = groups * capacity
    anywhere = pl.BlockSpec(memory_space=pl.ANY)
    return pl.pallas_call(
        expert_kernel,
        out_shape=jax.ShapeDtypeStruct(rows.shape, jnp.bfloat16),
        in_specs=[anywhere, anywhere, anywhere, anywhere],
        out_specs=pl.BlockSpec(memory_space=pltpu.VMEM),
        scratch_shapes=[
            pltpu.VMEM(rows.shape, rows.dtype),
            pltpu.VMEM(gate_local.shape, gate_local.dtype),
            pltpu.VMEM(up_local.shape, up_local.dtype),
            pltpu.VMEM(down_local.shape, down_local.dtype),
            pltpu.SemaphoreType.DMA((4, blocks)),
        ],
        compiler_params=pltpu.CompilerParams(vmem_limit_bytes=48 * 1024 * 1024),
        cost_estimate=pl.CostEstimate(
            flops=6 * row_count * blocks * width * hidden_units,
            transcendentals=row_count * hidden_units,
            bytes_accessed=2 * (2 * rows.size + gate_local.size + up_local.size + down_local.size),
        ),
    )(rows, gate_local, up_local, down_local)


def attend_local(queries, new_keys, new_values, key_cache, value_cache, lengths):
    request_count = queries.shape[0]
    group_size = QH // KVH
    score_scale = 1.0 / math.sqrt(HD)
    query_heads = queries.reshape(request_count, KVH, group_size, HD)
    head_eye = jnp.eye(KVH, dtype=queries.dtype)[None, :, None, :, None]
    spread_queries = (query_heads[:, :, :, None, :] * head_eye).reshape(request_count, QH, KVH * HD)
    scores = (
        jnp.einsum("rhc,rpc->rhp", spread_queries, key_cache, preferred_element_type=jnp.float32)
        * score_scale
    )
    score_new = (
        jnp.einsum("rhc,rc->rh", spread_queries, new_keys, preferred_element_type=jnp.float32)
        * score_scale
    )
    positions = jnp.arange(key_cache.shape[1], dtype=jnp.int32)
    live_mask = (positions[None, :] < lengths[:, None])[:, None, :]
    masked = jnp.where(live_mask, scores, FLOOR)
    largest = jnp.maximum(jnp.max(masked, axis=-1), score_new)
    weights = jnp.where(live_mask, jnp.exp(masked - largest[..., None]), 0.0)
    weight_new = jnp.exp(score_new - largest)
    denoms = jnp.sum(weights, axis=-1) + weight_new
    rounded_new = weight_new.astype(jnp.bfloat16).astype(jnp.float32)
    spread_totals = jnp.einsum(
        "rhp,rpc->rhc", weights.astype(jnp.bfloat16), value_cache, preferred_element_type=jnp.float32
    ) + rounded_new[..., None] * new_values[:, None, :].astype(jnp.float32)
    spread_totals = spread_totals / denoms[..., None]
    totals = jnp.sum(
        spread_totals.reshape(request_count, KVH, group_size, KVH, HD) * head_eye.astype(jnp.float32),
        axis=3,
    )
    return totals.astype(jnp.bfloat16).reshape(request_count, QH * HD)


def local(
    queries,
    new_keys,
    new_values,
    key_cache,
    value_cache,
    lengths,
    residual,
    out_weight,
    norm_gain,
    router,
    gate_weight,
    up_weight,
    down_weight,
    routes,
):
    attended = attend_local(queries, new_keys, new_values, key_cache, value_cache, lengths)
    gathered = gather_by_exchange(attended, "ffn").reshape(-1, attended.shape[1])
    hidden = residual.astype(jnp.float32) + jnp.dot(
        gathered,
        out_weight,
        preferred_element_type=jnp.float32,
    )
    scaled = hidden * norm_gain
    square_part = jnp.sum(hidden * hidden, axis=-1, keepdims=True)
    logit_part = jnp.dot(scaled, router, precision=lax.Precision.HIGHEST)
    stats = jnp.sum(
        gather_by_exchange(jnp.concatenate([square_part, logit_part], axis=1), "ffn"), axis=0
    )
    inverse = lax.rsqrt(stats[:, :1] / D + EPSILON)
    logits = stats[:, 1:] * inverse
    normed = (scaled * inverse).astype(jnp.bfloat16)
    expert_count = lax.axis_size("expert")
    row_count = routes.shape[0]
    capacity = row_count // 2
    expert_ids = jnp.arange(expert_count, dtype=jnp.int32)
    chosen = routes[:, :, None] == expert_ids[None, None, :]
    picked = jnp.sum(jnp.where(chosen, logits[:, None, :], 0.0), axis=-1)
    first_weight = jax.nn.sigmoid(picked[:, 0] - picked[:, 1])
    route_weights = jnp.stack([first_weight, 1.0 - first_weight], axis=1)
    flat_hits = chosen.astype(jnp.int32).reshape(row_count * 2, expert_count)
    earlier = jnp.cumsum(flat_hits, axis=0) - flat_hits
    slots = jnp.sum(earlier * flat_hits, axis=-1).reshape(row_count, 2)
    targets = routes * capacity + slots
    slot_ids = jnp.arange(expert_count * capacity, dtype=jnp.int32)
    slot_hits = slot_ids[:, None, None] == targets[None, :, :]
    dispatch = jnp.sum(slot_hits.astype(jnp.float32), axis=-1).astype(jnp.bfloat16)
    combine = jnp.sum(jnp.where(slot_hits, route_weights[None, :, :], 0.0), axis=-1).T
    gate_local = gate_weight[0]
    up_local = up_weight[0]
    down_local = down_weight[0]
    share_rows = (
        jnp.dot(dispatch, normed, preferred_element_type=jnp.float32)
        .astype(jnp.bfloat16)
        .reshape(expert_count, capacity, normed.shape[1])
    )
    feature_blocks = lax.axis_size("ffn")
    width = normed.shape[1]
    outgoing = jnp.broadcast_to(
        share_rows[:, None], (expert_count, feature_blocks, capacity, width)
    ).reshape(expert_count * feature_blocks, capacity, width)
    incoming = lax.all_to_all(outgoing, ("expert", "ffn"), 0, 0, tiled=True)
    partial_out = expert_block(
        incoming.reshape(expert_count, feature_blocks, capacity, width), gate_local, up_local, down_local
    ).reshape(expert_count * feature_blocks, capacity, width)
    pieces = lax.all_to_all(partial_out, ("expert", "ffn"), 0, 0, tiled=True)
    returned = (
        jnp.sum(pieces.reshape(expert_count, feature_blocks, capacity, width).astype(jnp.float32), axis=1)
        .astype(jnp.bfloat16)
    )
    mixed = jnp.dot(
        combine,
        returned.reshape(expert_count * capacity, -1).astype(jnp.float32),
        precision=lax.Precision.HIGHEST,
    )
    return (hidden + mixed).astype(jnp.bfloat16)


def solution(mesh):
    placed = (
        P(("expert", "ffn"), None),
        P(("expert", "ffn"), None),
        P(("expert", "ffn"), None),
        P(("expert", "ffn"), None, None),
        P(("expert", "ffn"), None, None),
        P(("expert", "ffn")),
        P("expert", "ffn"),
        P(None, "ffn"),
        P("ffn"),
        P("ffn", None),
        P("expert", None, "ffn"),
        P("expert", None, "ffn"),
        P("expert", "ffn", None),
        P("expert", None),
    )
    return jax.shard_map(
        local, mesh=mesh, in_specs=placed, out_specs=P("expert", "ffn"), check_vma=False
    )
```

```python
import math

import jax
import jax.numpy as jnp
from jax import lax
from jax.experimental import pallas as pl
from jax.experimental.pallas import tpu as pltpu
from jax.sharding import PartitionSpec as P

D = 4096
QH = 32
KVH = 8
HD = 128
CACHE = 512


EPSILON = 1e-05
FLOOR = -1e30


def butterfly_sum(value, axis_name):
    size = lax.axis_size(axis_name)
    step = 1
    while step < size:
        pairs = [(j, j ^ step) for j in range(size)]
        value = value + lax.ppermute(value, axis_name, pairs)
        step *= 2
    return value


def gather_by_exchange(value, axis_name):
    size = lax.axis_size(axis_name)
    copies = jnp.broadcast_to(value[None], (size,) + value.shape)
    return lax.all_to_all(copies, axis_name, 0, 0, tiled=True)


def expert_kernel(rows_hbm, gate_hbm, up_hbm, down_hbm, out_ref, rows_v, gate_v, up_v, down_v, sems):
    groups, blocks, capacity, width = rows_v.shape
    row_count = groups * capacity
    hidden_units = gate_v.shape[1]
    copies = []
    for block in range(blocks):
        span = pl.ds(block * width, width)
        trio = (
            pltpu.make_async_copy(rows_hbm.at[:, block], rows_v.at[:, block], sems.at[0, block]),
            pltpu.make_async_copy(gate_hbm.at[span], gate_v.at[span], sems.at[1, block]),
            pltpu.make_async_copy(up_hbm.at[span], up_v.at[span], sems.at[2, block]),
        )
        for copy in trio:
            copy.start()
        copies.append(trio)
    down_copy = pltpu.make_async_copy(down_hbm, down_v, sems.at[3, 0])
    down_copy.start()
    gate_sum = jnp.zeros((row_count, hidden_units), jnp.float32)
    up_sum = jnp.zeros((row_count, hidden_units), jnp.float32)
    for block in range(blocks):
        for copy in copies[block]:
            copy.wait()
        rows = rows_v[:, block].reshape(row_count, width)
        span = pl.ds(block * width, width)
        gate_sum += jnp.dot(rows, gate_v[span, :], preferred_element_type=jnp.float32)
        up_sum += jnp.dot(rows, up_v[span, :], preferred_element_type=jnp.float32)
    inner = (gate_sum / (1.0 + jnp.exp(-gate_sum)) * up_sum).astype(jnp.bfloat16)
    down_copy.wait()
    for block in range(blocks):
        part = jnp.dot(inner, down_v[:, pl.ds(block * width, width)], preferred_element_type=jnp.float32)
        out_ref[:, block] = part.astype(out_ref.dtype).reshape(groups, capacity, width)


def expert_block(rows, gate_local, up_local, down_local):
    groups, blocks, capacity, width = rows.shape
    hidden_units = gate_local.shape[1]
    row_count = groups * capacity
    anywhere = pl.BlockSpec(memory_space=pl.ANY)
    return pl.pallas_call(
        expert_kernel,
        out_shape=jax.ShapeDtypeStruct(rows.shape, jnp.bfloat16),
        in_specs=[anywhere, anywhere, anywhere, anywhere],
        out_specs=pl.BlockSpec(memory_space=pltpu.VMEM),
        scratch_shapes=[
            pltpu.VMEM(rows.shape, rows.dtype),
            pltpu.VMEM(gate_local.shape, gate_local.dtype),
            pltpu.VMEM(up_local.shape, up_local.dtype),
            pltpu.VMEM(down_local.shape, down_local.dtype),
            pltpu.SemaphoreType.DMA((4, blocks)),
        ],
        compiler_params=pltpu.CompilerParams(vmem_limit_bytes=48 * 1024 * 1024),
        cost_estimate=pl.CostEstimate(
            flops=6 * row_count * blocks * width * hidden_units,
            transcendentals=row_count * hidden_units,
            bytes_accessed=2 * (2 * rows.size + gate_local.size + up_local.size + down_local.size),
        ),
    )(rows, gate_local, up_local, down_local)


def attend_local(queries, new_keys, new_values, key_cache, value_cache, lengths):
    request_count = queries.shape[0]
    group_size = QH // KVH
    score_scale = 1.0 / math.sqrt(HD)
    query_heads = queries.reshape(request_count, KVH, group_size, HD)
    head_eye = jnp.eye(KVH, dtype=queries.dtype)[None, :, None, :, None]
    spread_queries = (query_heads[:, :, :, None, :] * head_eye).reshape(request_count, QH, KVH * HD)
    scores = (
        jnp.einsum("rpc,rhc->rph", key_cache, spread_queries, preferred_element_type=jnp.float32)
        * score_scale
    )
    score_new = (
        jnp.einsum("rhc,rc->rh", spread_queries, new_keys, preferred_element_type=jnp.float32)
        * score_scale
    )
    positions = jnp.arange(key_cache.shape[1], dtype=jnp.int32)
    live_mask = (positions[None, :] < lengths[:, None])[:, :, None]
    masked = jnp.where(live_mask, scores, FLOOR)
    largest = jnp.maximum(jnp.max(masked, axis=1), score_new)
    weights = jnp.where(live_mask, jnp.exp(masked - largest[:, None, :]), 0.0)
    weight_new = jnp.exp(score_new - largest)
    denoms = jnp.sum(weights, axis=1) + weight_new
    rounded_new = weight_new.astype(jnp.bfloat16).astype(jnp.float32)
    spread_totals = jnp.einsum(
        "rph,rpc->rhc", weights.astype(jnp.bfloat16), value_cache, preferred_element_type=jnp.float32
    ) + rounded_new[..., None] * new_values[:, None, :].astype(jnp.float32)
    spread_totals = spread_totals / denoms[..., None]
    totals = jnp.sum(
        spread_totals.reshape(request_count, KVH, group_size, KVH, HD) * head_eye.astype(jnp.float32),
        axis=3,
    )
    return totals.astype(jnp.bfloat16).reshape(request_count, QH * HD)


def local(
    queries,
    new_keys,
    new_values,
    key_cache,
    value_cache,
    lengths,
    residual,
    out_weight,
    norm_gain,
    router,
    gate_weight,
    up_weight,
    down_weight,
    routes,
):
    attended = attend_local(queries, new_keys, new_values, key_cache, value_cache, lengths)
    gathered = gather_by_exchange(attended, "ffn").reshape(-1, attended.shape[1])
    hidden = residual.astype(jnp.float32) + jnp.dot(
        gathered,
        out_weight,
        preferred_element_type=jnp.float32,
    )
    scaled = hidden * norm_gain
    square_part = jnp.sum(hidden * hidden, axis=-1, keepdims=True)
    logit_part = jnp.dot(scaled, router, precision=lax.Precision.HIGHEST)
    stats = jnp.sum(
        gather_by_exchange(jnp.concatenate([square_part, logit_part], axis=1), "ffn"), axis=0
    )
    inverse = lax.rsqrt(stats[:, :1] / D + EPSILON)
    logits = stats[:, 1:] * inverse
    normed = (scaled * inverse).astype(jnp.bfloat16)
    expert_count = lax.axis_size("expert")
    row_count = routes.shape[0]
    capacity = row_count // 2
    expert_ids = jnp.arange(expert_count, dtype=jnp.int32)
    chosen = routes[:, :, None] == expert_ids[None, None, :]
    picked = jnp.sum(jnp.where(chosen, logits[:, None, :], 0.0), axis=-1)
    first_weight = jax.nn.sigmoid(picked[:, 0] - picked[:, 1])
    route_weights = jnp.stack([first_weight, 1.0 - first_weight], axis=1)
    flat_hits = chosen.astype(jnp.int32).reshape(row_count * 2, expert_count)
    earlier = jnp.cumsum(flat_hits, axis=0) - flat_hits
    slots = jnp.sum(earlier * flat_hits, axis=-1).reshape(row_count, 2)
    targets = routes * capacity + slots
    slot_ids = jnp.arange(expert_count * capacity, dtype=jnp.int32)
    slot_hits = slot_ids[:, None, None] == targets[None, :, :]
    dispatch = jnp.sum(slot_hits.astype(jnp.float32), axis=-1).astype(jnp.bfloat16)
    combine = jnp.sum(jnp.where(slot_hits, route_weights[None, :, :], 0.0), axis=-1).T
    gate_local = gate_weight[0]
    up_local = up_weight[0]
    down_local = down_weight[0]
    share_rows = (
        jnp.dot(dispatch, normed, preferred_element_type=jnp.float32)
        .astype(jnp.bfloat16)
        .reshape(expert_count, capacity, normed.shape[1])
    )
    feature_blocks = lax.axis_size("ffn")
    width = normed.shape[1]
    outgoing = jnp.broadcast_to(
        share_rows[:, None], (expert_count, feature_blocks, capacity, width)
    ).reshape(expert_count * feature_blocks, capacity, width)
    incoming = lax.all_to_all(outgoing, ("expert", "ffn"), 0, 0, tiled=True)
    partial_out = expert_block(
        incoming.reshape(expert_count, feature_blocks, capacity, width), gate_local, up_local, down_local
    ).reshape(expert_count * feature_blocks, capacity, width)
    pieces = lax.all_to_all(partial_out, ("expert", "ffn"), 0, 0, tiled=True)
    returned = (
        jnp.sum(pieces.reshape(expert_count, feature_blocks, capacity, width).astype(jnp.float32), axis=1)
        .astype(jnp.bfloat16)
    )
    mixed = jnp.dot(
        combine,
        returned.reshape(expert_count * capacity, -1).astype(jnp.float32),
        precision=lax.Precision.HIGHEST,
    )
    return (hidden + mixed).astype(jnp.bfloat16)


def solution(mesh):
    placed = (
        P(("expert", "ffn"), None),
        P(("expert", "ffn"), None),
        P(("expert", "ffn"), None),
        P(("expert", "ffn"), None, None),
        P(("expert", "ffn"), None, None),
        P(("expert", "ffn")),
        P("expert", "ffn"),
        P(None, "ffn"),
        P("ffn"),
        P("ffn", None),
        P("expert", None, "ffn"),
        P("expert", None, "ffn"),
        P("expert", "ffn", None),
        P("expert", None),
    )
    return jax.shard_map(
        local, mesh=mesh, in_specs=placed, out_specs=P("expert", "ffn"), check_vma=False
    )
```

```python
import math

import jax
import jax.numpy as jnp
from jax import lax
from jax.experimental import pallas as pl
from jax.experimental.pallas import tpu as pltpu
from jax.sharding import PartitionSpec as P

D = 4096
QH = 32
KVH = 8
HD = 128
CACHE = 512


EPSILON = 1e-05
FLOOR = -1e30


def butterfly_sum(value, axis_name):
    size = lax.axis_size(axis_name)
    step = 1
    while step < size:
        pairs = [(j, j ^ step) for j in range(size)]
        value = value + lax.ppermute(value, axis_name, pairs)
        step *= 2
    return value


def gather_by_exchange(value, axis_name):
    size = lax.axis_size(axis_name)
    copies = jnp.broadcast_to(value[None], (size,) + value.shape)
    return lax.all_to_all(copies, axis_name, 0, 0, tiled=True)


def expert_kernel(rows_hbm, gate_hbm, up_hbm, down_hbm, out_ref, rows_v, gate_v, up_v, down_v, sems):
    groups, blocks, capacity, width = rows_v.shape
    row_count = groups * capacity
    hidden_units = gate_v.shape[1]
    rows_copy = pltpu.make_async_copy(rows_hbm, rows_v, sems.at[0, 0])
    rows_copy.start()
    copies = []
    for block in range(blocks):
        span = pl.ds(block * width, width)
        pair = (
            pltpu.make_async_copy(gate_hbm.at[span], gate_v.at[span], sems.at[1, block]),
            pltpu.make_async_copy(up_hbm.at[span], up_v.at[span], sems.at[2, block]),
        )
        for copy in pair:
            copy.start()
        copies.append(pair)
    down_copy = pltpu.make_async_copy(down_hbm, down_v, sems.at[3, 0])
    down_copy.start()
    gate_sum = jnp.zeros((row_count, hidden_units), jnp.float32)
    up_sum = jnp.zeros((row_count, hidden_units), jnp.float32)
    rows_copy.wait()
    for block in range(blocks):
        for copy in copies[block]:
            copy.wait()
        rows = rows_v[:, block].reshape(row_count, width)
        span = pl.ds(block * width, width)
        gate_sum += jnp.dot(rows, gate_v[span, :], preferred_element_type=jnp.float32)
        up_sum += jnp.dot(rows, up_v[span, :], preferred_element_type=jnp.float32)
    inner = (gate_sum / (1.0 + jnp.exp(-gate_sum)) * up_sum).astype(jnp.bfloat16)
    down_copy.wait()
    for block in range(blocks):
        part = jnp.dot(inner, down_v[:, pl.ds(block * width, width)], preferred_element_type=jnp.float32)
        out_ref[:, block] = part.astype(out_ref.dtype).reshape(groups, capacity, width)


def expert_block(rows, gate_local, up_local, down_local):
    groups, blocks, capacity, width = rows.shape
    hidden_units = gate_local.shape[1]
    row_count = groups * capacity
    anywhere = pl.BlockSpec(memory_space=pl.ANY)
    return pl.pallas_call(
        expert_kernel,
        out_shape=jax.ShapeDtypeStruct(rows.shape, jnp.bfloat16),
        in_specs=[anywhere, anywhere, anywhere, anywhere],
        out_specs=pl.BlockSpec(memory_space=pltpu.VMEM),
        scratch_shapes=[
            pltpu.VMEM(rows.shape, rows.dtype),
            pltpu.VMEM(gate_local.shape, gate_local.dtype),
            pltpu.VMEM(up_local.shape, up_local.dtype),
            pltpu.VMEM(down_local.shape, down_local.dtype),
            pltpu.SemaphoreType.DMA((4, blocks)),
        ],
        compiler_params=pltpu.CompilerParams(vmem_limit_bytes=48 * 1024 * 1024),
        cost_estimate=pl.CostEstimate(
            flops=6 * row_count * blocks * width * hidden_units,
            transcendentals=row_count * hidden_units,
            bytes_accessed=2 * (2 * rows.size + gate_local.size + up_local.size + down_local.size),
        ),
    )(rows, gate_local, up_local, down_local)


def attend_local(queries, new_keys, new_values, key_cache, value_cache, lengths):
    request_count = queries.shape[0]
    group_size = QH // KVH
    score_scale = 1.0 / math.sqrt(HD)
    query_heads = queries.reshape(request_count, KVH, group_size, HD)
    head_eye = jnp.eye(KVH, dtype=queries.dtype)[None, :, None, :, None]
    spread_queries = (query_heads[:, :, :, None, :] * head_eye).reshape(request_count, QH, KVH * HD)
    scores = (
        jnp.einsum("rhc,rpc->rhp", spread_queries, key_cache, preferred_element_type=jnp.float32)
        * score_scale
    )
    score_new = (
        jnp.einsum("rhc,rc->rh", spread_queries, new_keys, preferred_element_type=jnp.float32)
        * score_scale
    )
    positions = jnp.arange(key_cache.shape[1], dtype=jnp.int32)
    live_mask = (positions[None, :] < lengths[:, None])[:, None, :]
    masked = jnp.where(live_mask, scores, FLOOR)
    largest = jnp.maximum(jnp.max(masked, axis=-1), score_new)
    weights = jnp.where(live_mask, jnp.exp(masked - largest[..., None]), 0.0)
    weight_new = jnp.exp(score_new - largest)
    denoms = jnp.sum(weights, axis=-1) + weight_new
    rounded_new = weight_new.astype(jnp.bfloat16).astype(jnp.float32)
    spread_totals = jnp.einsum(
        "rhp,rpc->rhc", weights.astype(jnp.bfloat16), value_cache, preferred_element_type=jnp.float32
    ) + rounded_new[..., None] * new_values[:, None, :].astype(jnp.float32)
    spread_totals = spread_totals / denoms[..., None]
    totals = jnp.sum(
        spread_totals.reshape(request_count, KVH, group_size, KVH, HD) * head_eye.astype(jnp.float32),
        axis=3,
    )
    return totals.astype(jnp.bfloat16).reshape(request_count, QH * HD)


def local(
    queries,
    new_keys,
    new_values,
    key_cache,
    value_cache,
    lengths,
    residual,
    out_weight,
    norm_gain,
    router,
    gate_weight,
    up_weight,
    down_weight,
    routes,
):
    attended = attend_local(queries, new_keys, new_values, key_cache, value_cache, lengths)
    gathered = gather_by_exchange(attended, "ffn").reshape(-1, attended.shape[1])
    hidden = residual.astype(jnp.float32) + jnp.dot(
        gathered,
        out_weight,
        preferred_element_type=jnp.float32,
    )
    scaled = hidden * norm_gain
    square_part = jnp.sum(hidden * hidden, axis=-1, keepdims=True)
    logit_part = jnp.dot(scaled, router, precision=lax.Precision.HIGHEST)
    stats = jnp.sum(
        gather_by_exchange(jnp.concatenate([square_part, logit_part], axis=1), "ffn"), axis=0
    )
    inverse = lax.rsqrt(stats[:, :1] / D + EPSILON)
    logits = stats[:, 1:] * inverse
    normed = (scaled * inverse).astype(jnp.bfloat16)
    expert_count = lax.axis_size("expert")
    row_count = routes.shape[0]
    capacity = row_count // 2
    expert_ids = jnp.arange(expert_count, dtype=jnp.int32)
    chosen = routes[:, :, None] == expert_ids[None, None, :]
    picked = jnp.sum(jnp.where(chosen, logits[:, None, :], 0.0), axis=-1)
    first_weight = jax.nn.sigmoid(picked[:, 0] - picked[:, 1])
    route_weights = jnp.stack([first_weight, 1.0 - first_weight], axis=1)
    flat_hits = chosen.astype(jnp.int32).reshape(row_count * 2, expert_count)
    earlier = jnp.cumsum(flat_hits, axis=0) - flat_hits
    slots = jnp.sum(earlier * flat_hits, axis=-1).reshape(row_count, 2)
    targets = routes * capacity + slots
    slot_ids = jnp.arange(expert_count * capacity, dtype=jnp.int32)
    slot_hits = slot_ids[:, None, None] == targets[None, :, :]
    dispatch = jnp.sum(slot_hits.astype(jnp.float32), axis=-1).astype(jnp.bfloat16)
    combine = jnp.sum(jnp.where(slot_hits, route_weights[None, :, :], 0.0), axis=-1).T
    gate_local = gate_weight[0]
    up_local = up_weight[0]
    down_local = down_weight[0]
    share_rows = (
        jnp.dot(dispatch, normed, preferred_element_type=jnp.float32)
        .astype(jnp.bfloat16)
        .reshape(expert_count, capacity, normed.shape[1])
    )
    feature_blocks = lax.axis_size("ffn")
    width = normed.shape[1]
    outgoing = jnp.broadcast_to(
        share_rows[:, None], (expert_count, feature_blocks, capacity, width)
    ).reshape(expert_count * feature_blocks, capacity, width)
    incoming = lax.all_to_all(outgoing, ("expert", "ffn"), 0, 0, tiled=True)
    partial_out = expert_block(
        incoming.reshape(expert_count, feature_blocks, capacity, width), gate_local, up_local, down_local
    ).reshape(expert_count * feature_blocks, capacity, width)
    pieces = lax.all_to_all(partial_out, ("expert", "ffn"), 0, 0, tiled=True)
    returned = (
        jnp.sum(pieces.reshape(expert_count, feature_blocks, capacity, width).astype(jnp.float32), axis=1)
        .astype(jnp.bfloat16)
    )
    mixed = jnp.dot(
        combine,
        returned.reshape(expert_count * capacity, -1).astype(jnp.float32),
        precision=lax.Precision.HIGHEST,
    )
    return (hidden + mixed).astype(jnp.bfloat16)


def solution(mesh):
    placed = (
        P(("expert", "ffn"), None),
        P(("expert", "ffn"), None),
        P(("expert", "ffn"), None),
        P(("expert", "ffn"), None, None),
        P(("expert", "ffn"), None, None),
        P(("expert", "ffn")),
        P("expert", "ffn"),
        P(None, "ffn"),
        P("ffn"),
        P("ffn", None),
        P("expert", None, "ffn"),
        P("expert", None, "ffn"),
        P("expert", "ffn", None),
        P("expert", None),
    )
    return jax.shard_map(
        local, mesh=mesh, in_specs=placed, out_specs=P("expert", "ffn"), check_vma=False
    )
```
